32 devices in a mesh: tm: 4 (over y, x), chan: 8 (over z, core).
Axes of the slice: x: 2, y: 2, z: 4, core: 2. Of those that a mesh axis runs over, the one named last changes fastest.
Arguments:
- strain: bfloat16 [256, 16384], P('chan', 'tm'), may hold values from -6 to 6
- fir_taps: bfloat16 [256, 256], P('chan'), may hold values from -0.375 to 0.375
Outputs:
- stacked: float32 [2, 256, 256, 256], P(None, 'tm', 'chan')
The draws below stay inside these ranges and needn't reach their ends.
All inputs are finite; a program needn't handle non-finite values.
Results may differ from the reference program's by a relative error of at most 0.0062.
Values may be sent and summed in bfloat16 or wider, within the bound.
No kernel may reach another device: no remote copies, remote signals or barrier semaphores. Data moves between devices by JAX's collectives and lax.ppermute only.
A program may use at most 128 MiB of HBM per device.

```python
import math
import jax
import jax.numpy as jnp
from jax import lax

TAPS = 256
SEG = 512
BINS = 256
CHANNELS = 256
TIMES = 16384
NSEG = 32


def block_scale(own_key, dims, pieces, smallest, top_value):
    factor_of = 1.0
    for dim, parts in pieces:
        steps = jax.random.uniform(jax.random.fold_in(jax.random.fold_in(own_key, 6), dim), (parts,), jnp.float32, smallest / len(pieces), top_value / len(pieces))
        factor_of = factor_of * jnp.repeat(jnp.exp(steps), dims[dim] // parts).reshape((-1,) + (1,) * (len(dims) - 1 - dim))
    return factor_of


def centred(own_key, dims, scale, bound, cuts=(), held_as=jnp.bfloat16):
    drawn = jax.random.normal(own_key, dims, jnp.float32) * scale
    if len(cuts) > 0:
        drawn = block_scale(own_key, dims, cuts, -0.22, 0.18) * drawn
    return jnp.clip(drawn, min=-bound, max=bound).astype(held_as)


def setup_inputs(seed: int = 0) -> dict:
    splits = jax.random.split(jax.random.key(seed), 3)
    strain = centred(splits[0], (CHANNELS, TIMES), 1.0, 6.0, ((0, 8), (1, 4)))
    fir_taps = centred(splits[1], (CHANNELS, TAPS), TAPS ** -0.5, 0.375, ((0, 8),))
    return dict(strain=strain, fir_taps=fir_taps)


def make_table():
    sample_idx = jnp.arange(SEG, dtype=jnp.int32)
    bin_idx = jnp.arange(BINS, dtype=jnp.int32)
    phases = (sample_idx[:, None] * bin_idx[None, :]) % SEG
    angles = phases.astype(jnp.float32) * (2.0 * math.pi / SEG)
    window = 0.5 - 0.5 * jnp.cos(sample_idx.astype(jnp.float32) * (2.0 * math.pi / SEG))
    cosine = window[:, None] * jnp.cos(angles)
    sine_part = -window[:, None] * jnp.sin(angles)
    return jnp.stack([cosine, sine_part], axis=1).astype(jnp.bfloat16)


def toeplitz(fir_taps):
    tap_count = fir_taps.shape[1]
    row_idx = jnp.arange(2 * tap_count, dtype=jnp.int32)[:, None]
    col_idx = jnp.arange(tap_count, dtype=jnp.int32)[None, :]
    lag_idx = col_idx + tap_count - row_idx
    valid = (lag_idx >= 0) & (lag_idx < tap_count)
    picked = jnp.take(fir_taps, jnp.clip(lag_idx, 0, tap_count - 1).astype(jnp.int32), axis=1)
    return jnp.where(valid[None, :, :], picked, jnp.zeros_like(picked))


def cross_block(own_bins, other_bins):
    own_wide = own_bins.astype(jnp.float32)
    other_wide = other_bins.astype(jnp.float32)
    swapped = jnp.stack([-other_wide[:, 1], other_wide[:, 0]], axis=1)
    real_part = jnp.einsum("kpsi,kpsj->kij", own_wide, other_wide, precision=lax.Precision.HIGHEST)
    imag_part = jnp.einsum("kpsi,kpsj->kij", own_wide, swapped, precision=lax.Precision.HIGHEST)
    return jnp.stack([real_part, imag_part], axis=0)


def reference(strain, fir_taps):
    channels = strain.shape[0]
    matrix = toeplitz(fir_taps).astype(jnp.float32)
    extended = jnp.concatenate([jnp.zeros((channels, TAPS), strain.dtype), strain], axis=1)
    blocks = extended.reshape(channels, -1, TAPS).astype(jnp.float32)
    block_pairs = jnp.concatenate([blocks[:, :-1], blocks[:, 1:]], axis=2)
    filtered = jnp.einsum("cbr,cri->cbi", block_pairs, matrix, precision=lax.Precision.HIGHEST)
    whitened = filtered.reshape(channels, -1).astype(jnp.bfloat16)
    segments = whitened.reshape(channels, NSEG, SEG).astype(jnp.float32)
    table = make_table().astype(jnp.float32)
    spectra = jnp.einsum("csn,npk->kpsc", segments, table, precision=lax.Precision.HIGHEST).astype(jnp.bfloat16)
    grouped = spectra.reshape(BINS // 16, 16, 2, NSEG, channels)
    stacks = lax.map(lambda group: cross_block(group, group), grouped)
    stacked = jnp.transpose(stacks, (1, 0, 2, 3, 4)).reshape(2, BINS, channels, channels)
    return stacked * (1.0 / (NSEG * SEG))
```

```python
import math

import jax
import jax.numpy as jnp
from jax import lax
from jax.sharding import PartitionSpec as P

SEG = 512


def shifted(value, axis, by):
    size = lax.axis_size(axis)
    pairs = [(i, i + by) for i in range(size) if 0 <= i + by < size]
    return lax.ppermute(value, axis, pairs)


def make_table():
    sample_idx = jnp.arange(SEG, dtype=jnp.int32)
    bin_idx = jnp.arange(SEG // 2, dtype=jnp.int32)
    phases = sample_idx[:, None] * bin_idx[None, :] % SEG
    angles = phases.astype(jnp.float32) * (2.0 * math.pi / SEG)
    window = 0.5 - 0.5 * jnp.cos(sample_idx.astype(jnp.float32) * (2.0 * math.pi / SEG))
    cosine = window[:, None] * jnp.cos(angles)
    sine_part = -window[:, None] * jnp.sin(angles)
    return jnp.stack([cosine, sine_part], axis=1).astype(jnp.bfloat16)


def toeplitz(fir_taps):
    tap_count = fir_taps.shape[1]
    row_idx = jnp.arange(2 * tap_count, dtype=jnp.int32)[:, None]
    col_idx = jnp.arange(tap_count, dtype=jnp.int32)[None, :]
    lag_idx = col_idx + tap_count - row_idx
    valid = (lag_idx >= 0) & (lag_idx < tap_count)
    picked = jnp.take(fir_taps, jnp.clip(lag_idx, 0, tap_count - 1), axis=1)
    return jnp.where(valid[None, :, :], picked, jnp.zeros_like(picked))


def cross_block(own_bins, other_bins):
    swapped = jnp.stack([-other_bins[:, 1], other_bins[:, 0]], axis=1)
    real_part = jnp.einsum(
        "kpsi,kpsj->kij", own_bins, other_bins, preferred_element_type=jnp.float32
    )
    imag_part = jnp.einsum("kpsi,kpsj->kij", own_bins, swapped, preferred_element_type=jnp.float32)
    return jnp.stack([real_part, imag_part], axis=0)


def shards(strain, fir_taps):
    tap_count = fir_taps.shape[1]
    channels = strain.shape[0]
    previous = shifted(strain[:, -tap_count:], "tm", 1)
    extended = jnp.concatenate([previous, strain], axis=1)[:, 1:]
    filtered = lax.conv_general_dilated(
        extended[None],
        jnp.flip(fir_taps, axis=1)[:, None, :],
        window_strides=(1,),
        padding="VALID",
        dimension_numbers=("NCH", "OIH", "NCH"),
        feature_group_count=channels,
        preferred_element_type=jnp.float32,
    )[0]
    whitened = filtered.reshape(channels, -1).astype(jnp.bfloat16)
    segments = whitened.reshape(channels, whitened.shape[1] // SEG, SEG)
    spectra = jnp.einsum(
        "csn,npk->kpsc", segments, make_table(), preferred_element_type=jnp.float32
    ).astype(jnp.bfloat16)
    gathered = lax.all_gather(spectra, "chan", axis=3, tiled=True)
    all_bins = lax.all_to_all(gathered, "tm", split_axis=0, concat_axis=2, tiled=True)
    factor = 1.0 / (all_bins.shape[2] * SEG)
    first_col = lax.axis_index("chan") * channels
    own_bins = lax.dynamic_slice_in_dim(all_bins, first_col, channels, 3)
    result = cross_block(own_bins, all_bins) * factor
    return result


def solution(mesh):
    placed = (P("chan", "tm"), P("chan", None))
    return jax.shard_map(
        shards, mesh=mesh, in_specs=placed, out_specs=P(None, "tm", "chan", None), check_vma=False
    )
```

```python
import math

import jax
import jax.numpy as jnp
from jax import lax
from jax.sharding import PartitionSpec as P

SEG = 512


def shifted(value, axis, by):
    size = lax.axis_size(axis)
    pairs = [(i, i + by) for i in range(size) if 0 <= i + by < size]
    return lax.ppermute(value, axis, pairs)


def make_table():
    sample_idx = jnp.arange(SEG, dtype=jnp.int32)
    bin_idx = jnp.arange(SEG // 2, dtype=jnp.int32)
    phases = sample_idx[:, None] * bin_idx[None, :] % SEG
    angles = phases.astype(jnp.float32) * (2.0 * math.pi / SEG)
    window = 0.5 - 0.5 * jnp.cos(sample_idx.astype(jnp.float32) * (2.0 * math.pi / SEG))
    cosine = window[:, None] * jnp.cos(angles)
    sine_part = -window[:, None] * jnp.sin(angles)
    return jnp.stack([cosine, sine_part], axis=1).astype(jnp.bfloat16)


def toeplitz(fir_taps):
    tap_count = fir_taps.shape[1]
    row_idx = jnp.arange(2 * tap_count, dtype=jnp.int32)[:, None]
    col_idx = jnp.arange(tap_count, dtype=jnp.int32)[None, :]
    lag_idx = col_idx + tap_count - row_idx
    valid = (lag_idx >= 0) & (lag_idx < tap_count)
    picked = jnp.take(fir_taps, jnp.clip(lag_idx, 0, tap_count - 1), axis=1)
    return jnp.where(valid[None, :, :], picked, jnp.zeros_like(picked))


def cross_block(own_bins, other_bins):
    swapped = jnp.stack([-other_bins[:, 1], other_bins[:, 0]], axis=1)
    real_part = jnp.einsum(
        "kpsi,kpsj->kij", own_bins, other_bins, preferred_element_type=jnp.float32
    )
    imag_part = jnp.einsum("kpsi,kpsj->kij", own_bins, swapped, preferred_element_type=jnp.float32)
    return jnp.stack([real_part, imag_part], axis=0)


def shards(strain, fir_taps):
    tap_count = fir_taps.shape[1]
    channels = strain.shape[0]
    previous = shifted(strain[:, -tap_count:], "tm", 1)
    extended = jnp.concatenate([previous, strain], axis=1)[:, 1:]
    filtered = lax.conv_general_dilated(
        extended[None],
        jnp.flip(fir_taps, axis=1)[:, None, :],
        window_strides=(1,),
        padding="VALID",
        dimension_numbers=("NCH", "OIH", "NCH"),
        feature_group_count=channels,
        preferred_element_type=jnp.float32,
    )[0]
    whitened = filtered.reshape(channels, -1).astype(jnp.bfloat16)
    segments = whitened.reshape(channels, whitened.shape[1] // SEG, SEG)
    spectra = jnp.einsum(
        "csn,npk->kpsc", segments, make_table(), preferred_element_type=jnp.float32
    ).astype(jnp.bfloat16)
    own_bins = lax.all_to_all(spectra, "tm", split_axis=0, concat_axis=2, tiled=True)
    all_bins = lax.all_gather(own_bins, "chan", axis=3, tiled=True)
    factor = 1.0 / (all_bins.shape[2] * SEG)
    result = cross_block(own_bins, all_bins) * factor
    return result


def solution(mesh):
    placed = (P("chan", "tm"), P("chan", None))
    return jax.shard_map(
        shards, mesh=mesh, in_specs=placed, out_specs=P(None, "tm", "chan", None), check_vma=False
    )
```

```python
import math

import jax
import jax.numpy as jnp
from jax import lax
from jax.sharding import PartitionSpec as P

SEG = 512


def shifted(value, axis, by):
    size = lax.axis_size(axis)
    pairs = [(i, i + by) for i in range(size) if 0 <= i + by < size]
    return lax.ppermute(value, axis, pairs)


def make_table():
    sample_idx = jnp.arange(SEG, dtype=jnp.int32)
    bin_idx = jnp.arange(SEG // 2, dtype=jnp.int32)
    phases = sample_idx[:, None] * bin_idx[None, :] % SEG
    angles = phases.astype(jnp.float32) * (2.0 * math.pi / SEG)
    window = 0.5 - 0.5 * jnp.cos(sample_idx.astype(jnp.float32) * (2.0 * math.pi / SEG))
    cosine = window[:, None] * jnp.cos(angles)
    sine_part = -window[:, None] * jnp.sin(angles)
    return jnp.stack([cosine, sine_part], axis=1).astype(jnp.bfloat16)


def toeplitz(fir_taps):
    tap_count = fir_taps.shape[1]
    row_idx = jnp.arange(2 * tap_count, dtype=jnp.int32)[:, None]
    col_idx = jnp.arange(tap_count, dtype=jnp.int32)[None, :]
    lag_idx = col_idx + tap_count - row_idx
    valid = (lag_idx >= 0) & (lag_idx < tap_count)
    picked = jnp.take(fir_taps, jnp.clip(lag_idx, 0, tap_count - 1), axis=1)
    return jnp.where(valid[None, :, :], picked, jnp.zeros_like(picked))


def cross_block(own_bins, other_bins):
    swapped = jnp.stack([-other_bins[:, 1], other_bins[:, 0]], axis=1)
    real_part = jnp.einsum(
        "kpsi,kpsj->kij", own_bins, other_bins, preferred_element_type=jnp.float32
    )
    imag_part = jnp.einsum("kpsi,kpsj->kij", own_bins, swapped, preferred_element_type=jnp.float32)
    return jnp.stack([real_part, imag_part], axis=0)


def shards(strain, fir_taps):
    tap_count = fir_taps.shape[1]
    channels = strain.shape[0]
    previous = shifted(strain[:, -tap_count:], "tm", 1)
    extended = jnp.concatenate([previous, strain], axis=1)
    blocks = extended.reshape(channels, -1, tap_count)
    block_pairs = jnp.concatenate([blocks[:, :-1], blocks[:, 1:]], axis=2)
    padded_taps = jnp.pad(fir_taps, ((0, 0), (tap_count - 1, tap_count)))
    windows = lax.conv_general_dilated_patches(
        padded_taps[:, None, :], (2 * tap_count,), (1,), "VALID"
    )
    filtered = jnp.einsum(
        "cbw,cwi->cbi",
        jnp.flip(block_pairs, axis=2),
        windows,
        preferred_element_type=jnp.float32,
    )
    whitened = filtered.reshape(channels, -1).astype(jnp.bfloat16)
    segments = whitened.reshape(channels, whitened.shape[1] // SEG, SEG)
    spectra = jnp.einsum(
        "csn,npk->kpsc", segments, make_table(), preferred_element_type=jnp.float32
    ).astype(jnp.bfloat16)
    own_bins = lax.all_to_all(spectra, "tm", split_axis=0, concat_axis=2, tiled=True)
    all_bins = lax.all_gather(own_bins, "chan", axis=3, tiled=True)
    factor = 1.0 / (all_bins.shape[2] * SEG)
    result = cross_block(own_bins, all_bins) * factor
    return result


def solution(mesh):
    placed = (P("chan", "tm"), P("chan", None))
    return jax.shard_map(
        shards, mesh=mesh, in_specs=placed, out_specs=P(None, "tm", "chan", None), check_vma=False
    )
```

```python
import math

import jax
import jax.numpy as jnp
from jax import lax
from jax.experimental import pallas as pl
from jax.experimental.pallas import tpu as pltpu
from jax.sharding import PartitionSpec as P

SEG = 512


def shifted(value, axis, by):
    size = lax.axis_size(axis)
    pairs = [(i, i + by) for i in range(size) if 0 <= i + by < size]
    return lax.ppermute(value, axis, pairs)


def make_table():
    sample_idx = jnp.arange(SEG, dtype=jnp.int32)
    bin_idx = jnp.arange(SEG // 2, dtype=jnp.int32)
    phases = sample_idx[:, None] * bin_idx[None, :] % SEG
    angles = phases.astype(jnp.float32) * (2.0 * math.pi / SEG)
    window = 0.5 - 0.5 * jnp.cos(sample_idx.astype(jnp.float32) * (2.0 * math.pi / SEG))
    cosine = window[:, None] * jnp.cos(angles)
    sine_part = -window[:, None] * jnp.sin(angles)
    return jnp.stack([cosine, sine_part], axis=1).astype(jnp.bfloat16)


def toeplitz(fir_taps):
    tap_count = fir_taps.shape[1]
    row_idx = jnp.arange(2 * tap_count, dtype=jnp.int32)[:, None]
    col_idx = jnp.arange(tap_count, dtype=jnp.int32)[None, :]
    lag_idx = col_idx + tap_count - row_idx
    valid = (lag_idx >= 0) & (lag_idx < tap_count)
    picked = jnp.take(fir_taps, jnp.clip(lag_idx, 0, tap_count - 1), axis=1)
    return jnp.where(valid[None, :, :], picked, jnp.zeros_like(picked))


def cross_block(own_bins, other_bins):
    swapped = jnp.stack([-other_bins[:, 1], other_bins[:, 0]], axis=1)
    real_part = jnp.einsum(
        "kpsi,kpsj->kij", own_bins, other_bins, preferred_element_type=jnp.float32
    )
    imag_part = jnp.einsum("kpsi,kpsj->kij", own_bins, swapped, preferred_element_type=jnp.float32)
    return jnp.stack([real_part, imag_part], axis=0)


def fir_kernel(taps_ref, early_ref, late_ref, out_ref):
    half = taps_ref.shape[1] // 2
    row = lax.broadcasted_iota(jnp.int32, (half, half), 0)
    col = lax.broadcasted_iota(jnp.int32, (half, half), 1)
    upper = col >= row
    zero = jnp.zeros((half, half), jnp.float32)
    for ci in range(taps_ref.shape[0]):
        taps = taps_ref[pl.ds(ci, 1), :].astype(jnp.float32)
        low = jnp.broadcast_to(taps[:, :half], (half, half))
        high = jnp.broadcast_to(taps[:, half:], (half, half))
        low = pltpu.roll(low, 0, 1, stride=1, stride_axis=0)
        high = pltpu.roll(high, 0, 1, stride=1, stride_axis=0)
        d0 = jnp.where(upper, zero, high).astype(jnp.bfloat16)
        d1 = jnp.where(upper, high, low).astype(jnp.bfloat16)
        d2 = jnp.where(upper, low, zero).astype(jnp.bfloat16)
        none = jnp.zeros_like(d0)
        top = jnp.concatenate(
            [jnp.concatenate([d0, none], axis=1), jnp.concatenate([d1, d0], axis=1)], axis=0
        )
        bottom = jnp.concatenate(
            [jnp.concatenate([d2, d1], axis=1), jnp.concatenate([none, d2], axis=1)], axis=0
        )
        acc = jnp.dot(early_ref[ci], top, preferred_element_type=jnp.float32)
        acc = acc + jnp.dot(late_ref[ci], bottom, preferred_element_type=jnp.float32)
        out_ref[ci] = acc.astype(out_ref.dtype)


def whiten(fir_taps, early, late):
    channels, nblocks, tap_count = late.shape
    group = 8
    block = pl.BlockSpec((group, nblocks, tap_count), lambda g: (g, 0, 0))
    return pl.pallas_call(
        fir_kernel,
        out_shape=jax.ShapeDtypeStruct(late.shape, jnp.bfloat16),
        grid=(channels // group,),
        in_specs=[pl.BlockSpec((group, tap_count), lambda g: (g, 0)), block, block],
        out_specs=block,
        cost_estimate=pl.CostEstimate(
            flops=4 * channels * nblocks * tap_count * tap_count,
            bytes_accessed=3 * late.size * 2 + fir_taps.size * 2,
            transcendentals=0,
        ),
    )(fir_taps, early, late)


def shards(strain, fir_taps):
    tap_count = fir_taps.shape[1]
    channels = strain.shape[0]
    previous = shifted(strain[:, -tap_count:], "tm", 1)
    early = jnp.concatenate([previous, strain[:, :-tap_count]], axis=1)
    early = early.reshape(channels, -1, tap_count)
    late = strain.reshape(channels, -1, tap_count)
    whitened = whiten(fir_taps, early, late).reshape(channels, -1)
    segments = whitened.reshape(channels, whitened.shape[1] // SEG, SEG)
    spectra = jnp.einsum(
        "csn,npk->kpsc", segments, make_table(), preferred_element_type=jnp.float32
    ).astype(jnp.bfloat16)
    own_bins = lax.all_to_all(spectra, "tm", split_axis=0, concat_axis=2, tiled=True)
    all_bins = lax.all_gather(own_bins, "chan", axis=3, tiled=True)
    factor = 1.0 / (all_bins.shape[2] * SEG)
    result = cross_block(own_bins, all_bins) * factor
    return result


def solution(mesh):
    placed = (P("chan", "tm"), P("chan", None))
    return jax.shard_map(
        shards, mesh=mesh, in_specs=placed, out_specs=P(None, "tm", "chan", None), check_vma=False
    )
```

```python
import math

import jax
import jax.numpy as jnp
from jax import lax
from jax.experimental import pallas as pl
from jax.experimental.pallas import tpu as pltpu
from jax.sharding import PartitionSpec as P

SEG = 512


def shifted(value, axis, by):
    size = lax.axis_size(axis)
    pairs = [(i, i + by) for i in range(size) if 0 <= i + by < size]
    return lax.ppermute(value, axis, pairs)


def make_table():
    sample_idx = jnp.arange(SEG, dtype=jnp.int32)
    bin_idx = jnp.arange(SEG // 2, dtype=jnp.int32)
    phases = sample_idx[:, None] * bin_idx[None, :] % SEG
    angles = phases.astype(jnp.float32) * (2.0 * math.pi / SEG)
    window = 0.5 - 0.5 * jnp.cos(sample_idx.astype(jnp.float32) * (2.0 * math.pi / SEG))
    cosine = window[:, None] * jnp.cos(angles)
    sine_part = -window[:, None] * jnp.sin(angles)
    return jnp.stack([cosine, sine_part], axis=1).astype(jnp.bfloat16)


def toeplitz(fir_taps):
    tap_count = fir_taps.shape[1]
    row_idx = jnp.arange(2 * tap_count, dtype=jnp.int32)[:, None]
    col_idx = jnp.arange(tap_count, dtype=jnp.int32)[None, :]
    lag_idx = col_idx + tap_count - row_idx
    valid = (lag_idx >= 0) & (lag_idx < tap_count)
    picked = jnp.take(fir_taps, jnp.clip(lag_idx, 0, tap_count - 1), axis=1)
    return jnp.where(valid[None, :, :], picked, jnp.zeros_like(picked))


def cross_block(own_bins, other_bins):
    swapped = jnp.stack([-other_bins[:, 1], other_bins[:, 0]], axis=1)
    real_part = jnp.einsum(
        "kpsi,kpsj->kij", own_bins, other_bins, preferred_element_type=jnp.float32
    )
    imag_part = jnp.einsum("kpsi,kpsj->kij", own_bins, swapped, preferred_element_type=jnp.float32)
    return jnp.stack([real_part, imag_part], axis=0)


def fir_kernel(taps_ref, early_ref, late_ref, out_ref):
    half = taps_ref.shape[1] // 2
    row = lax.broadcasted_iota(jnp.int32, (half, half), 0)
    col = lax.broadcasted_iota(jnp.int32, (half, half), 1)
    upper = col >= row
    zero = jnp.zeros((half, half), jnp.float32)
    for ci in range(taps_ref.shape[0]):
        taps = taps_ref[pl.ds(ci, 1), :].astype(jnp.float32)
        low = jnp.broadcast_to(taps[:, :half], (half, half))
        high = jnp.broadcast_to(taps[:, half:], (half, half))
        low = pltpu.roll(low, 0, 1, stride=1, stride_axis=0)
        high = pltpu.roll(high, 0, 1, stride=1, stride_axis=0)
        d0 = jnp.where(upper, zero, high).astype(jnp.bfloat16)
        d1 = jnp.where(upper, high, low).astype(jnp.bfloat16)
        d2 = jnp.where(upper, low, zero).astype(jnp.bfloat16)
        none = jnp.zeros_like(d0)
        top = jnp.concatenate(
            [jnp.concatenate([d0, none], axis=1), jnp.concatenate([d1, d0], axis=1)], axis=0
        )
        bottom = jnp.concatenate(
            [jnp.concatenate([d2, d1], axis=1), jnp.concatenate([none, d2], axis=1)], axis=0
        )
        acc = jnp.dot(early_ref[ci], top, preferred_element_type=jnp.float32)
        acc = acc + jnp.dot(late_ref[ci], bottom, preferred_element_type=jnp.float32)
        out_ref[ci] = acc.astype(out_ref.dtype)


def whiten(fir_taps, early, late):
    channels, nblocks, tap_count = late.shape
    group = 8
    block = pl.BlockSpec((group, nblocks, tap_count), lambda g: (g, 0, 0))
    return pl.pallas_call(
        fir_kernel,
        out_shape=jax.ShapeDtypeStruct(late.shape, jnp.bfloat16),
        grid=(channels // group,),
        in_specs=[pl.BlockSpec((group, tap_count), lambda g: (g, 0)), block, block],
        out_specs=block,
        cost_estimate=pl.CostEstimate(
            flops=4 * channels * nblocks * tap_count * tap_count,
            bytes_accessed=3 * late.size * 2 + fir_taps.size * 2,
            transcendentals=0,
        ),
    )(fir_taps, early, late)


def shards(strain, fir_taps):
    tap_count = fir_taps.shape[1]
    channels = strain.shape[0]
    previous = shifted(strain[:, -tap_count:], "tm", 1)
    early = jnp.concatenate([previous, strain[:, :-tap_count]], axis=1)
    early = early.reshape(channels, -1, tap_count)
    late = strain.reshape(channels, -1, tap_count)
    whitened = whiten(fir_taps, early, late).reshape(channels, -1)
    segments = whitened.reshape(channels, whitened.shape[1] // SEG, SEG)
    spectra = jnp.einsum(
        "csn,npk->kpsc", segments, make_table(), preferred_element_type=jnp.float32
    ).astype(jnp.bfloat16)
    return cross_spectra(spectra)


def permuted(value, axis, pairs):
    return lax.ppermute(value, axis, [(a, b) for a, b in pairs])


def exchange_bins(spectra):
    size = lax.axis_size("tm")
    me = lax.axis_index("tm")
    pieces = spectra.reshape((size, spectra.shape[0] // size) + spectra.shape[1:])
    received = [pieces[me]]
    for m in range(1, size):
        piece = lax.dynamic_index_in_dim(pieces, me ^ m, 0, keepdims=False)
        received.append(permuted(piece, "tm", [(i, i ^ m) for i in range(size)]))
    return jnp.stack(received, axis=0)


def gather_channels(shard):
    size = lax.axis_size("chan")
    chips = size // 2
    me = lax.axis_index("chan")
    chip, core = me // 2, me % 2
    right = [(c * 2 + k, (c + 1) * 2 + k) for c in range(chips - 1) for k in range(2)]
    left = [(b, a) for a, b in right]
    from_left, from_right = [None], [None]
    going_right, going_left = shard, shard
    for _ in range(1, chips):
        going_right = permuted(going_right, "chan", right)
        going_left = permuted(going_left, "chan", left)
        from_left.append(going_right)
        from_right.append(going_left)
    rotated = [shard]
    for u in range(1, chips):
        rotated.append(jnp.where(chip + u < chips, from_right[u], from_left[chips - u]))
    rotated = jnp.stack(rotated, axis=0)
    doubled = jnp.concatenate([rotated, rotated], axis=0)
    mine = lax.dynamic_slice_in_dim(doubled, chips - chip, chips, axis=0)
    other = permuted(mine, "chan", [(i, i ^ 1) for i in range(size)])
    first = jnp.where(core == 0, mine, other)
    second = jnp.where(core == 0, other, mine)
    return jnp.stack([first, second], axis=1)


def cross_spectra(spectra):
    own = exchange_bins(spectra)
    every = gather_channels(own)
    wide = every.shape[0] * every.shape[1] * every.shape[-1]
    swapped = jnp.stack([-every[:, :, :, :, 1], every[:, :, :, :, 0]], axis=4)
    real_part = jnp.einsum("ukpsi,qrukpsj->kiqrj", own, every, preferred_element_type=jnp.float32)
    imag_part = jnp.einsum("ukpsi,qrukpsj->kiqrj", own, swapped, preferred_element_type=jnp.float32)
    result = jnp.stack([real_part, imag_part], axis=0)
    result = result.reshape(result.shape[:3] + (wide,))
    factor = 1.0 / (own.shape[0] * own.shape[3] * SEG)
    return result * factor


def solution(mesh):
    placed = (P("chan", "tm"), P("chan", None))
    return jax.shard_map(
        shards, mesh=mesh, in_specs=placed, out_specs=P(None, "tm", "chan", None), check_vma=False
    )
```

```python
import math

import jax
import jax.numpy as jnp
from jax import lax
from jax.experimental import pallas as pl
from jax.experimental.pallas import tpu as pltpu
from jax.sharding import PartitionSpec as P

SEG = 512


def shifted(value, axis, by):
    size = lax.axis_size(axis)
    pairs = [(i, i + by) for i in range(size) if 0 <= i + by < size]
    return lax.ppermute(value, axis, pairs)


def make_table():
    sample_idx = jnp.arange(SEG, dtype=jnp.int32)
    bin_idx = jnp.arange(SEG // 2, dtype=jnp.int32)
    phases = sample_idx[:, None] * bin_idx[None, :] % SEG
    angles = phases.astype(jnp.float32) * (2.0 * math.pi / SEG)
    window = 0.5 - 0.5 * jnp.cos(sample_idx.astype(jnp.float32) * (2.0 * math.pi / SEG))
    cosine = window[:, None] * jnp.cos(angles)
    sine_part = -window[:, None] * jnp.sin(angles)
    return jnp.stack([cosine, sine_part], axis=1).astype(jnp.bfloat16)


def toeplitz(fir_taps):
    tap_count = fir_taps.shape[1]
    row_idx = jnp.arange(2 * tap_count, dtype=jnp.int32)[:, None]
    col_idx = jnp.arange(tap_count, dtype=jnp.int32)[None, :]
    lag_idx = col_idx + tap_count - row_idx
    valid = (lag_idx >= 0) & (lag_idx < tap_count)
    picked = jnp.take(fir_taps, jnp.clip(lag_idx, 0, tap_count - 1), axis=1)
    return jnp.where(valid[None, :, :], picked, jnp.zeros_like(picked))


def cross_block(own_bins, other_bins):
    swapped = jnp.stack([-other_bins[:, 1], other_bins[:, 0]], axis=1)
    real_part = jnp.einsum(
        "kpsi,kpsj->kij", own_bins, other_bins, preferred_element_type=jnp.float32
    )
    imag_part = jnp.einsum("kpsi,kpsj->kij", own_bins, swapped, preferred_element_type=jnp.float32)
    return jnp.stack([real_part, imag_part], axis=0)


def fir_kernel(taps_ref, early_ref, late_ref, out_ref):
    half = taps_ref.shape[1] // 2
    row = lax.broadcasted_iota(jnp.int32, (half, half), 0)
    col = lax.broadcasted_iota(jnp.int32, (half, half), 1)
    upper = col >= row
    zero = jnp.zeros((half, half), jnp.float32)
    for ci in range(taps_ref.shape[0]):
        taps = taps_ref[pl.ds(ci, 1), :].astype(jnp.float32)
        low = jnp.broadcast_to(taps[:, :half], (half, half))
        high = jnp.broadcast_to(taps[:, half:], (half, half))
        low = pltpu.roll(low, 0, 1, stride=1, stride_axis=0)
        high = pltpu.roll(high, 0, 1, stride=1, stride_axis=0)
        d0 = jnp.where(upper, zero, high).astype(jnp.bfloat16)
        d1 = jnp.where(upper, high, low).astype(jnp.bfloat16)
        d2 = jnp.where(upper, low, zero).astype(jnp.bfloat16)
        none = jnp.zeros_like(d0)
        top = jnp.concatenate(
            [jnp.concatenate([d0, none], axis=1), jnp.concatenate([d1, d0], axis=1)], axis=0
        )
        bottom = jnp.concatenate(
            [jnp.concatenate([d2, d1], axis=1), jnp.concatenate([none, d2], axis=1)], axis=0
        )
        acc = jnp.dot(early_ref[ci], top, preferred_element_type=jnp.float32)
        acc = acc + jnp.dot(late_ref[ci], bottom, preferred_element_type=jnp.float32)
        out_ref[ci] = acc.astype(out_ref.dtype)


def whiten(fir_taps, early, late):
    channels, nblocks, tap_count = late.shape
    group = 8
    block = pl.BlockSpec((group, nblocks, tap_count), lambda g: (g, 0, 0))
    return pl.pallas_call(
        fir_kernel,
        out_shape=jax.ShapeDtypeStruct(late.shape, jnp.bfloat16),
        grid=(channels // group,),
        in_specs=[pl.BlockSpec((group, tap_count), lambda g: (g, 0)), block, block],
        out_specs=block,
        cost_estimate=pl.CostEstimate(
            flops=4 * channels * nblocks * tap_count * tap_count,
            bytes_accessed=3 * late.size * 2 + fir_taps.size * 2,
            transcendentals=0,
        ),
    )(fir_taps, early, late)


def shards(strain, fir_taps):
    tap_count = fir_taps.shape[1]
    channels = strain.shape[0]
    previous = shifted(strain[:, -tap_count:], "tm", 1)
    early = jnp.concatenate([previous, strain[:, :-tap_count]], axis=1)
    early = early.reshape(channels, -1, tap_count)
    late = strain.reshape(channels, -1, tap_count)
    whitened = whiten(fir_taps, early, late).reshape(channels, -1)
    segments = whitened.reshape(channels * (whitened.shape[1] // SEG), SEG)
    parts = lax.axis_size("tm")
    table = make_table()
    bins = table.shape[2]
    table = table.reshape(SEG, 2, parts, bins // parts).transpose(0, 2, 1, 3).reshape(SEG, 2 * bins)
    spectra = jnp.einsum(
        "xn,nq->qx", segments, table, preferred_element_type=jnp.float32
    ).astype(jnp.bfloat16)
    spectra = spectra.reshape(parts, spectra.shape[0] // parts, spectra.shape[1])
    own = lax.all_to_all(spectra, "tm", split_axis=0, concat_axis=0, tiled=True)
    every = lax.all_gather(own, "chan", axis=0)
    own = own.reshape(parts, 2, bins // parts, channels, -1)
    every = every.reshape(every.shape[:2] + (2, bins // parts, channels, -1))
    swapped = jnp.stack([-every[:, :, 1], every[:, :, 0]], axis=2)
    real_part = jnp.einsum("upkis,Jupkjs->kiJj", own, every, preferred_element_type=jnp.float32)
    imag_part = jnp.einsum("upkis,Jupkjs->kiJj", own, swapped, preferred_element_type=jnp.float32)
    result = jnp.stack([real_part, imag_part], axis=0)
    result = result.reshape(result.shape[:3] + (-1,))
    factor = 1.0 / (parts * own.shape[-1] * SEG)
    return result * factor


def solution(mesh):
    placed = (P("chan", "tm"), P("chan", None))
    return jax.shard_map(
        shards, mesh=mesh, in_specs=placed, out_specs=P(None, "tm", "chan", None), check_vma=False
    )
```

```python
import math

import jax
import jax.numpy as jnp
from jax import lax
from jax.experimental import pallas as pl
from jax.experimental.pallas import tpu as pltpu
from jax.sharding import PartitionSpec as P

SEG = 512


def shifted(value, axis, by):
    size = lax.axis_size(axis)
    pairs = [(i, i + by) for i in range(size) if 0 <= i + by < size]
    return lax.ppermute(value, axis, pairs)


def make_table():
    sample_idx = jnp.arange(SEG, dtype=jnp.int32)
    bin_idx = jnp.arange(SEG // 2, dtype=jnp.int32)
    phases = sample_idx[:, None] * bin_idx[None, :] % SEG
    angles = phases.astype(jnp.float32) * (2.0 * math.pi / SEG)
    window = 0.5 - 0.5 * jnp.cos(sample_idx.astype(jnp.float32) * (2.0 * math.pi / SEG))
    cosine = window[:, None] * jnp.cos(angles)
    sine_part = -window[:, None] * jnp.sin(angles)
    return jnp.stack([cosine, sine_part], axis=1).astype(jnp.bfloat16)


def toeplitz(fir_taps):
    tap_count = fir_taps.shape[1]
    row_idx = jnp.arange(2 * tap_count, dtype=jnp.int32)[:, None]
    col_idx = jnp.arange(tap_count, dtype=jnp.int32)[None, :]
    lag_idx = col_idx + tap_count - row_idx
    valid = (lag_idx >= 0) & (lag_idx < tap_count)
    picked = jnp.take(fir_taps, jnp.clip(lag_idx, 0, tap_count - 1), axis=1)
    return jnp.where(valid[None, :, :], picked, jnp.zeros_like(picked))


def cross_block(own_bins, other_bins):
    swapped = jnp.stack([-other_bins[:, 1], other_bins[:, 0]], axis=1)
    real_part = jnp.einsum(
        "kpsi,kpsj->kij", own_bins, other_bins, preferred_element_type=jnp.float32
    )
    imag_part = jnp.einsum("kpsi,kpsj->kij", own_bins, swapped, preferred_element_type=jnp.float32)
    return jnp.stack([real_part, imag_part], axis=0)


def fir_kernel(taps_ref, early_ref, late_ref, out_ref):
    half = taps_ref.shape[1] // 2
    row = lax.broadcasted_iota(jnp.int32, (half, half), 0)
    col = lax.broadcasted_iota(jnp.int32, (half, half), 1)
    upper = col >= row
    zero = jnp.zeros((half, half), jnp.float32)
    for ci in range(taps_ref.shape[0]):
        taps = taps_ref[pl.ds(ci, 1), :].astype(jnp.float32)
        low = jnp.broadcast_to(taps[:, :half], (half, half))
        high = jnp.broadcast_to(taps[:, half:], (half, half))
        low = pltpu.roll(low, 0, 1, stride=1, stride_axis=0)
        high = pltpu.roll(high, 0, 1, stride=1, stride_axis=0)
        d0 = jnp.where(upper, zero, high).astype(jnp.bfloat16)
        d1 = jnp.where(upper, high, low).astype(jnp.bfloat16)
        d2 = jnp.where(upper, low, zero).astype(jnp.bfloat16)
        none = jnp.zeros_like(d0)
        top = jnp.concatenate(
            [jnp.concatenate([d0, none], axis=1), jnp.concatenate([d1, d0], axis=1)], axis=0
        )
        bottom = jnp.concatenate(
            [jnp.concatenate([d2, d1], axis=1), jnp.concatenate([none, d2], axis=1)], axis=0
        )
        acc = jnp.dot(early_ref[ci], top, preferred_element_type=jnp.float32)
        acc = acc + jnp.dot(late_ref[ci], bottom, preferred_element_type=jnp.float32)
        out_ref[ci] = acc.astype(out_ref.dtype)


def whiten(fir_taps, early, late):
    channels, nblocks, tap_count = late.shape
    group = 8
    block = pl.BlockSpec((group, nblocks, tap_count), lambda g: (g, 0, 0))
    return pl.pallas_call(
        fir_kernel,
        out_shape=jax.ShapeDtypeStruct(late.shape, jnp.bfloat16),
        grid=(channels // group,),
        in_specs=[pl.BlockSpec((group, tap_count), lambda g: (g, 0)), block, block],
        out_specs=block,
        cost_estimate=pl.CostEstimate(
            flops=4 * channels * nblocks * tap_count * tap_count,
            bytes_accessed=3 * late.size * 2 + fir_taps.size * 2,
            transcendentals=0,
        ),
    )(fir_taps, early, late)


def shards(strain, fir_taps):
    tap_count = fir_taps.shape[1]
    channels = strain.shape[0]
    previous = shifted(strain[:, -tap_count:], "tm", 1)
    early = jnp.concatenate([previous, strain[:, :-tap_count]], axis=1)
    early = early.reshape(channels, -1, tap_count)
    late = strain.reshape(channels, -1, tap_count)
    whitened = whiten(fir_taps, early, late).reshape(channels, -1)
    segments = whitened.reshape(channels * (whitened.shape[1] // SEG), SEG)
    parts = lax.axis_size("tm")
    table = make_table()
    bins = table.shape[2]
    table = table.reshape(SEG, 2, parts, bins // parts).transpose(0, 2, 1, 3).reshape(SEG, 2 * bins)
    spectra = jnp.einsum(
        "xn,nq->qx", segments, table, preferred_element_type=jnp.float32
    ).astype(jnp.bfloat16)
    spectra = spectra.reshape(parts, spectra.shape[0] // parts, spectra.shape[1])
    own = lax.all_to_all(spectra, "tm", split_axis=0, concat_axis=0, tiled=True)
    pairs = bins // parts // 2
    shard = own.reshape(parts, 2, pairs, 2, channels, -1).transpose(2, 4, 3, 1, 0, 5)
    shard = shard.reshape(pairs, channels, -1)
    every = lax.all_gather(shard, "chan", axis=0)
    return cross_spectra(lhs_rows(shard), every)


def lhs_rows(shard):
    pairs, channels, lanes = shard.shape
    split = shard.reshape(pairs, channels, 2, 2, lanes // 4)
    parity = lax.broadcasted_iota(jnp.int32, split.shape, 2)
    zero = jnp.zeros_like(split)
    swapped = jnp.concatenate([split[:, :, :, 1:], -split[:, :, :, :1]], axis=3)
    rows = []
    for part in (split, swapped):
        for b in range(2):
            rows.append(jnp.where(parity == b, part, zero).reshape(pairs, channels, lanes))
    return jnp.stack(rows, axis=1).reshape(pairs, 4 * channels, lanes)


def cross_kernel(lhs_ref, every_ref, out_ref):
    sources, count, channels, lanes = every_ref.shape
    factor = 1.0 / (lanes // 4 * SEG)
    for t in range(count):
        rhs = every_ref[:, t].reshape(sources * channels, lanes)
        prod = lax.dot_general(
            lhs_ref[t], rhs, (((1,), (1,)), ((), ())), preferred_element_type=jnp.float32
        )
        prod = prod * factor
        for q in range(4):
            out_ref[q // 2, 2 * t + q % 2] = prod[q * channels:(q + 1) * channels]


def cross_spectra(lhs, every):
    sources, pairs, channels, lanes = every.shape
    step = 8 if pairs % 8 == 0 else pairs
    wide = sources * channels
    return pl.pallas_call(
        cross_kernel,
        out_shape=jax.ShapeDtypeStruct((2, 2 * pairs, channels, wide), jnp.float32),
        grid=(pairs // step,),
        in_specs=[
            pl.BlockSpec((step, 4 * channels, lanes), lambda g: (g, 0, 0)),
            pl.BlockSpec((sources, step, channels, lanes), lambda g: (0, g, 0, 0)),
        ],
        out_specs=pl.BlockSpec((2, 2 * step, channels, wide), lambda g: (0, g, 0, 0)),
        cost_estimate=pl.CostEstimate(
            flops=2 * pairs * 4 * channels * lanes * wide,
            bytes_accessed=lhs.size * 2 + every.size * 2 + 2 * 2 * pairs * channels * wide * 4,
            transcendentals=0,
        ),
    )(lhs, every)


def solution(mesh):
    placed = (P("chan", "tm"), P("chan", None))
    return jax.shard_map(
        shards, mesh=mesh, in_specs=placed, out_specs=P(None, "tm", "chan", None), check_vma=False
    )
```

```python
import math

import jax
import ml_dtypes
import numpy as np
import jax.numpy as jnp
from jax import lax
from jax.experimental import pallas as pl
from jax.experimental.pallas import tpu as pltpu
from jax.sharding import Mesh, PartitionSpec as P

SEG = 512


def shifted(value, axis, by):
    size = lax.axis_size(axis)
    pairs = [(i, i + by) for i in range(size) if 0 <= i + by < size]
    return lax.ppermute(value, axis, pairs)


def make_table():
    sample_idx = np.arange(SEG, dtype=np.int32)
    bin_idx = np.arange(SEG // 2, dtype=np.int32)
    phases = sample_idx[:, None] * bin_idx[None, :] % SEG
    step = np.float32(2.0 * math.pi / SEG)
    angles = phases.astype(np.float32) * step
    window = np.float32(0.5) - np.float32(0.5) * np.cos(sample_idx.astype(np.float32) * step)
    cosine = window[:, None] * np.cos(angles)
    sine_part = -window[:, None] * np.sin(angles)
    return np.stack([cosine, sine_part], axis=1).astype(ml_dtypes.bfloat16)


def toeplitz(fir_taps):
    tap_count = fir_taps.shape[1]
    row_idx = jnp.arange(2 * tap_count, dtype=jnp.int32)[:, None]
    col_idx = jnp.arange(tap_count, dtype=jnp.int32)[None, :]
    lag_idx = col_idx + tap_count - row_idx
    valid = (lag_idx >= 0) & (lag_idx < tap_count)
    picked = jnp.take(fir_taps, jnp.clip(lag_idx, 0, tap_count - 1), axis=1)
    return jnp.where(valid[None, :, :], picked, jnp.zeros_like(picked))


def cross_block(own_bins, other_bins):
    swapped = jnp.stack([-other_bins[:, 1], other_bins[:, 0]], axis=1)
    real_part = jnp.einsum(
        "kpsi,kpsj->kij", own_bins, other_bins, preferred_element_type=jnp.float32
    )
    imag_part = jnp.einsum("kpsi,kpsj->kij", own_bins, swapped, preferred_element_type=jnp.float32)
    return jnp.stack([real_part, imag_part], axis=0)


def fir_kernel(taps_ref, early_ref, late_ref, out_ref):
    half = taps_ref.shape[1] // 2
    row = lax.broadcasted_iota(jnp.int32, (half, half), 0)
    col = lax.broadcasted_iota(jnp.int32, (half, half), 1)
    upper = col >= row
    zero = jnp.zeros((half, half), jnp.float32)
    for ci in range(taps_ref.shape[0]):
        taps = taps_ref[pl.ds(ci, 1), :].astype(jnp.float32)
        low = jnp.broadcast_to(taps[:, :half], (half, half))
        high = jnp.broadcast_to(taps[:, half:], (half, half))
        low = pltpu.roll(low, 0, 1, stride=1, stride_axis=0)
        high = pltpu.roll(high, 0, 1, stride=1, stride_axis=0)
        d0 = jnp.where(upper, zero, high).astype(jnp.bfloat16)
        d1 = jnp.where(upper, high, low).astype(jnp.bfloat16)
        d2 = jnp.where(upper, low, zero).astype(jnp.bfloat16)
        none = jnp.zeros_like(d0)
        top = jnp.concatenate(
            [jnp.concatenate([d0, none], axis=1), jnp.concatenate([d1, d0], axis=1)], axis=0
        )
        bottom = jnp.concatenate(
            [jnp.concatenate([d2, d1], axis=1), jnp.concatenate([none, d2], axis=1)], axis=0
        )
        acc = jnp.dot(early_ref[ci], top, preferred_element_type=jnp.float32)
        acc = acc + jnp.dot(late_ref[ci], bottom, preferred_element_type=jnp.float32)
        out_ref[ci] = acc.astype(out_ref.dtype)


def whiten(fir_taps, early, late):
    channels, nblocks, tap_count = late.shape
    group = 8
    block = pl.BlockSpec((group, nblocks, tap_count), lambda g: (g, 0, 0))
    return pl.pallas_call(
        fir_kernel,
        out_shape=jax.ShapeDtypeStruct(late.shape, jnp.bfloat16),
        grid=(channels // group,),
        in_specs=[pl.BlockSpec((group, tap_count), lambda g: (g, 0)), block, block],
        out_specs=block,
        cost_estimate=pl.CostEstimate(
            flops=4 * channels * nblocks * tap_count * tap_count,
            bytes_accessed=3 * late.size * 2 + fir_taps.size * 2,
            transcendentals=0,
        ),
    )(fir_taps, early, late)


def shards(strain, fir_taps):
    tap_count = fir_taps.shape[1]
    channels = strain.shape[0]
    previous = shifted(strain[:, -tap_count:], "tm", 1)
    early = jnp.concatenate([previous, strain[:, :-tap_count]], axis=1)
    early = early.reshape(channels, -1, tap_count)
    late = strain.reshape(channels, -1, tap_count)
    whitened = whiten(fir_taps, early, late).reshape(channels, -1)
    segments = whitened.reshape(channels * (whitened.shape[1] // SEG), SEG)
    parts = lax.axis_size("tm")
    table = make_table()
    bins = table.shape[2]
    table = jnp.asarray(
        table.reshape(SEG, 2, parts, bins // parts).transpose(0, 2, 1, 3).reshape(SEG, 2 * bins)
    )
    spectra = jnp.einsum(
        "xn,nq->qx", segments, table, preferred_element_type=jnp.float32
    ).astype(jnp.bfloat16)
    spectra = spectra.reshape(parts, spectra.shape[0] // parts, spectra.shape[1])
    own = lax.all_to_all(spectra, "tm", split_axis=0, concat_axis=0, tiled=True)
    pairs = bins // parts // 2
    shard = own.reshape(parts, 2, pairs, 2, channels, -1).transpose(2, 4, 3, 1, 0, 5)
    shard = shard.reshape(pairs, channels, -1)
    every = lax.all_gather(shard, "chip", axis=0)
    every = lax.all_gather(every, "core", axis=1)
    every = every.reshape((-1,) + shard.shape)
    return cross_spectra(lhs_rows(shard), every)


def lhs_rows(shard):
    pairs, channels, lanes = shard.shape
    split = shard.reshape(pairs, channels, 2, 2, lanes // 4)
    parity = lax.broadcasted_iota(jnp.int32, split.shape, 2)
    zero = jnp.zeros_like(split)
    swapped = jnp.concatenate([split[:, :, :, 1:], -split[:, :, :, :1]], axis=3)
    rows = []
    for part in (split, swapped):
        for b in range(2):
            rows.append(jnp.where(parity == b, part, zero).reshape(pairs, channels, lanes))
    return jnp.stack(rows, axis=1).reshape(pairs, 4 * channels, lanes)


def cross_kernel(lhs_ref, every_ref, out_ref):
    sources, count, channels, lanes = every_ref.shape
    factor = 1.0 / (lanes // 4 * SEG)
    for t in range(count):
        rhs = every_ref[:, t].reshape(sources * channels, lanes)
        prod = lax.dot_general(
            lhs_ref[t], rhs, (((1,), (1,)), ((), ())), preferred_element_type=jnp.float32
        )
        prod = prod * factor
        for q in range(4):
            out_ref[q // 2, 2 * t + q % 2] = prod[q * channels:(q + 1) * channels]


def cross_spectra(lhs, every):
    sources, pairs, channels, lanes = every.shape
    step = 8 if pairs % 8 == 0 else pairs
    wide = sources * channels
    return pl.pallas_call(
        cross_kernel,
        out_shape=jax.ShapeDtypeStruct((2, 2 * pairs, channels, wide), jnp.float32),
        grid=(pairs // step,),
        in_specs=[
            pl.BlockSpec((step, 4 * channels, lanes), lambda g: (g, 0, 0)),
            pl.BlockSpec((sources, step, channels, lanes), lambda g: (0, g, 0, 0)),
        ],
        out_specs=pl.BlockSpec((2, 2 * step, channels, wide), lambda g: (0, g, 0, 0)),
        cost_estimate=pl.CostEstimate(
            flops=2 * pairs * 4 * channels * lanes * wide,
            bytes_accessed=lhs.size * 2 + every.size * 2 + 2 * 2 * pairs * channels * wide * 4,
            transcendentals=0,
        ),
    )(lhs, every)


def solution(mesh):
    tm_size, chan_size = mesh.devices.shape
    split = Mesh(mesh.devices.reshape(tm_size, chan_size // 2, 2), ("tm", "chip", "core"))
    chan = ("chip", "core")
    placed = (P(chan, "tm"), P(chan, None))
    return jax.shard_map(
        shards, mesh=split, in_specs=placed, out_specs=P(None, "tm", chan, None), check_vma=False
    )
```

```python
import math

import jax
import ml_dtypes
import numpy as np
import jax.numpy as jnp
from jax import lax
from jax.experimental import pallas as pl
from jax.experimental.pallas import tpu as pltpu
from jax.sharding import PartitionSpec as P

SEG = 512


def shifted(value, axis, by):
    size = lax.axis_size(axis)
    pairs = [(i, i + by) for i in range(size) if 0 <= i + by < size]
    return lax.ppermute(value, axis, pairs)


def make_table():
    sample_idx = np.arange(SEG, dtype=np.int32)
    bin_idx = np.arange(SEG // 2, dtype=np.int32)
    phases = sample_idx[:, None] * bin_idx[None, :] % SEG
    step = np.float32(2.0 * math.pi / SEG)
    angles = phases.astype(np.float32) * step
    window = np.float32(0.5) - np.float32(0.5) * np.cos(sample_idx.astype(np.float32) * step)
    cosine = window[:, None] * np.cos(angles)
    sine_part = -window[:, None] * np.sin(angles)
    return np.stack([cosine, sine_part], axis=1).astype(ml_dtypes.bfloat16)


def toeplitz(fir_taps):
    tap_count = fir_taps.shape[1]
    row_idx = jnp.arange(2 * tap_count, dtype=jnp.int32)[:, None]
    col_idx = jnp.arange(tap_count, dtype=jnp.int32)[None, :]
    lag_idx = col_idx + tap_count - row_idx
    valid = (lag_idx >= 0) & (lag_idx < tap_count)
    picked = jnp.take(fir_taps, jnp.clip(lag_idx, 0, tap_count - 1), axis=1)
    return jnp.where(valid[None, :, :], picked, jnp.zeros_like(picked))


def cross_block(own_bins, other_bins):
    swapped = jnp.stack([-other_bins[:, 1], other_bins[:, 0]], axis=1)
    real_part = jnp.einsum(
        "kpsi,kpsj->kij", own_bins, other_bins, preferred_element_type=jnp.float32
    )
    imag_part = jnp.einsum("kpsi,kpsj->kij", own_bins, swapped, preferred_element_type=jnp.float32)
    return jnp.stack([real_part, imag_part], axis=0)


def fir_kernel(taps_ref, early_ref, late_ref, out_ref):
    half = taps_ref.shape[1] // 2
    row = lax.broadcasted_iota(jnp.int32, (half, half), 0)
    col = lax.broadcasted_iota(jnp.int32, (half, half), 1)
    upper = col >= row
    zero = jnp.zeros((half, half), jnp.float32)
    for ci in range(taps_ref.shape[0]):
        taps = taps_ref[pl.ds(ci, 1), :].astype(jnp.float32)
        low = jnp.broadcast_to(taps[:, :half], (half, half))
        high = jnp.broadcast_to(taps[:, half:], (half, half))
        low = pltpu.roll(low, 0, 1, stride=1, stride_axis=0)
        high = pltpu.roll(high, 0, 1, stride=1, stride_axis=0)
        d0 = jnp.where(upper, zero, high).astype(jnp.bfloat16)
        d1 = jnp.where(upper, high, low).astype(jnp.bfloat16)
        d2 = jnp.where(upper, low, zero).astype(jnp.bfloat16)
        none = jnp.zeros_like(d0)
        top = jnp.concatenate(
            [jnp.concatenate([d0, none], axis=1), jnp.concatenate([d1, d0], axis=1)], axis=0
        )
        bottom = jnp.concatenate(
            [jnp.concatenate([d2, d1], axis=1), jnp.concatenate([none, d2], axis=1)], axis=0
        )
        acc = jnp.dot(early_ref[ci], top, preferred_element_type=jnp.float32)
        acc = acc + jnp.dot(late_ref[ci], bottom, preferred_element_type=jnp.float32)
        out_ref[ci] = acc.astype(out_ref.dtype)


def whiten(fir_taps, early, late):
    channels, nblocks, tap_count = late.shape
    group = 8
    block = pl.BlockSpec((group, nblocks, tap_count), lambda g: (g, 0, 0))
    return pl.pallas_call(
        fir_kernel,
        out_shape=jax.ShapeDtypeStruct(late.shape, jnp.bfloat16),
        grid=(channels // group,),
        in_specs=[pl.BlockSpec((group, tap_count), lambda g: (g, 0)), block, block],
        out_specs=block,
        cost_estimate=pl.CostEstimate(
            flops=4 * channels * nblocks * tap_count * tap_count,
            bytes_accessed=3 * late.size * 2 + fir_taps.size * 2,
            transcendentals=0,
        ),
    )(fir_taps, early, late)


def shards(strain, fir_taps):
    tap_count = fir_taps.shape[1]
    channels = strain.shape[0]
    previous = shifted(strain[:, -tap_count:], "tm", 1)
    early = jnp.concatenate([previous, strain[:, :-tap_count]], axis=1)
    early = early.reshape(channels, -1, tap_count)
    late = strain.reshape(channels, -1, tap_count)
    whitened = whiten(fir_taps, early, late).reshape(channels, -1)
    segments = whitened.reshape(channels * (whitened.shape[1] // SEG), SEG)
    parts = lax.axis_size("tm")
    table = make_table()
    bins = table.shape[2]
    table = jnp.asarray(
        table.reshape(SEG, 2, parts, bins // parts).transpose(0, 2, 1, 3).reshape(SEG, 2 * bins)
    )
    spectra = jnp.einsum(
        "xn,nq->qx", segments, table, preferred_element_type=jnp.float32
    ).astype(jnp.bfloat16)
    spectra = spectra.reshape(parts, spectra.shape[0] // parts, spectra.shape[1])
    own = lax.all_to_all(spectra, "tm", split_axis=0, concat_axis=0, tiled=True)
    pairs = bins // parts // 2
    split = own.reshape(parts, 2, pairs, 2, channels, -1)
    chunks = 2 if pairs % 16 == 0 else 1
    size = pairs // chunks
    result = None
    for h in range(chunks):
        shard = split[:, :, h * size:(h + 1) * size].transpose(2, 4, 3, 1, 0, 5)
        shard = shard.reshape(size, channels, -1)
        every = lax.all_gather(shard, "chan", axis=0)
        result = cross_spectra(lhs_rows(shard), every, pairs, h * size, result)
    return result


def lhs_rows(shard):
    pairs, channels, lanes = shard.shape
    split = shard.reshape(pairs, channels, 2, 2, lanes // 4)
    parity = lax.broadcasted_iota(jnp.int32, split.shape, 2)
    zero = jnp.zeros_like(split)
    swapped = jnp.concatenate([split[:, :, :, 1:], -split[:, :, :, :1]], axis=3)
    rows = []
    for part in (split, swapped):
        for b in range(2):
            rows.append(jnp.where(parity == b, part, zero).reshape(pairs, channels, lanes))
    return jnp.stack(rows, axis=1).reshape(pairs, 4 * channels, lanes)


def cross_kernel(lhs_ref, every_ref, out_ref):
    sources, count, channels, lanes = every_ref.shape
    factor = 1.0 / (lanes // 4 * SEG)
    for t in range(count):
        rhs = every_ref[:, t].reshape(sources * channels, lanes)
        prod = lax.dot_general(
            lhs_ref[t], rhs, (((1,), (1,)), ((), ())), preferred_element_type=jnp.float32
        )
        prod = prod * factor
        for q in range(4):
            out_ref[q // 2, 2 * t + q % 2] = prod[q * channels:(q + 1) * channels]


def cross_spectra(lhs, every, total, start, result):
    sources, pairs, channels, lanes = every.shape
    step = 8 if pairs % 8 == 0 else pairs
    wide = sources * channels
    first = start // step
    operands = (lhs, every) if result is None else (lhs, every, result)
    specs = [
        pl.BlockSpec((step, 4 * channels, lanes), lambda g: (g, 0, 0)),
        pl.BlockSpec((sources, step, channels, lanes), lambda g: (0, g, 0, 0)),
    ]
    if result is not None:
        specs.append(pl.BlockSpec(memory_space=pl.ANY))
    return pl.pallas_call(
        cross_kernel if result is None else cross_kernel_into,
        out_shape=jax.ShapeDtypeStruct((2, 2 * total, channels, wide), jnp.float32),
        grid=(pairs // step,),
        in_specs=specs,
        out_specs=pl.BlockSpec((2, 2 * step, channels, wide), lambda g: (0, g + first, 0, 0)),
        input_output_aliases={} if result is None else {2: 0},
        cost_estimate=pl.CostEstimate(
            flops=2 * pairs * 4 * channels * lanes * wide,
            bytes_accessed=lhs.size * 2 + every.size * 2 + 2 * 2 * pairs * channels * wide * 4,
            transcendentals=0,
        ),
    )(*operands)


def cross_kernel_into(lhs_ref, every_ref, result_ref, out_ref):
    cross_kernel(lhs_ref, every_ref, out_ref)


def solution(mesh):
    placed = (P("chan", "tm"), P("chan", None))
    return jax.shard_map(
        shards, mesh=mesh, in_specs=placed, out_specs=P(None, "tm", "chan", None), check_vma=False
    )
```

```python
import math

import jax
import ml_dtypes
import numpy as np
import jax.numpy as jnp
from jax import lax
from jax.experimental import pallas as pl
from jax.experimental.pallas import tpu as pltpu
from jax.sharding import PartitionSpec as P

SEG = 512


def shifted(value, axis, by):
    size = lax.axis_size(axis)
    pairs = [(i, i + by) for i in range(size) if 0 <= i + by < size]
    return lax.ppermute(value, axis, pairs)


def make_table():
    sample_idx = np.arange(SEG, dtype=np.int32)
    bin_idx = np.arange(SEG // 2, dtype=np.int32)
    phases = sample_idx[:, None] * bin_idx[None, :] % SEG
    step = np.float32(2.0 * math.pi / SEG)
    angles = phases.astype(np.float32) * step
    window = np.float32(0.5) - np.float32(0.5) * np.cos(sample_idx.astype(np.float32) * step)
    cosine = window[:, None] * np.cos(angles)
    sine_part = -window[:, None] * np.sin(angles)
    return np.stack([cosine, sine_part], axis=1).astype(ml_dtypes.bfloat16)


def toeplitz(fir_taps):
    tap_count = fir_taps.shape[1]
    row_idx = jnp.arange(2 * tap_count, dtype=jnp.int32)[:, None]
    col_idx = jnp.arange(tap_count, dtype=jnp.int32)[None, :]
    lag_idx = col_idx + tap_count - row_idx
    valid = (lag_idx >= 0) & (lag_idx < tap_count)
    picked = jnp.take(fir_taps, jnp.clip(lag_idx, 0, tap_count - 1), axis=1)
    return jnp.where(valid[None, :, :], picked, jnp.zeros_like(picked))


def cross_block(own_bins, other_bins):
    swapped = jnp.stack([-other_bins[:, 1], other_bins[:, 0]], axis=1)
    real_part = jnp.einsum(
        "kpsi,kpsj->kij", own_bins, other_bins, preferred_element_type=jnp.float32
    )
    imag_part = jnp.einsum("kpsi,kpsj->kij", own_bins, swapped, preferred_element_type=jnp.float32)
    return jnp.stack([real_part, imag_part], axis=0)


def fir_kernel(taps_ref, early_ref, late_ref, out_ref):
    half = taps_ref.shape[1] // 2
    row = lax.broadcasted_iota(jnp.int32, (half, half), 0)
    col = lax.broadcasted_iota(jnp.int32, (half, half), 1)
    upper = col >= row
    zero = jnp.zeros((half, half), jnp.float32)
    for ci in range(taps_ref.shape[0]):
        taps = taps_ref[pl.ds(ci, 1), :].astype(jnp.float32)
        low = jnp.broadcast_to(taps[:, :half], (half, half))
        high = jnp.broadcast_to(taps[:, half:], (half, half))
        low = pltpu.roll(low, 0, 1, stride=1, stride_axis=0)
        high = pltpu.roll(high, 0, 1, stride=1, stride_axis=0)
        d0 = jnp.where(upper, zero, high).astype(jnp.bfloat16)
        d1 = jnp.where(upper, high, low).astype(jnp.bfloat16)
        d2 = jnp.where(upper, low, zero).astype(jnp.bfloat16)
        none = jnp.zeros_like(d0)
        top = jnp.concatenate(
            [jnp.concatenate([d0, none], axis=1), jnp.concatenate([d1, d0], axis=1)], axis=0
        )
        bottom = jnp.concatenate(
            [jnp.concatenate([d2, d1], axis=1), jnp.concatenate([none, d2], axis=1)], axis=0
        )
        acc = jnp.dot(early_ref[ci], top, preferred_element_type=jnp.float32)
        acc = acc + jnp.dot(late_ref[ci], bottom, preferred_element_type=jnp.float32)
        out_ref[ci] = acc.astype(out_ref.dtype)


def whiten(fir_taps, early, late):
    channels, nblocks, tap_count = late.shape
    group = 8
    block = pl.BlockSpec((group, nblocks, tap_count), lambda g: (g, 0, 0))
    return pl.pallas_call(
        fir_kernel,
        out_shape=jax.ShapeDtypeStruct(late.shape, jnp.bfloat16),
        grid=(channels // group,),
        in_specs=[pl.BlockSpec((group, tap_count), lambda g: (g, 0)), block, block],
        out_specs=block,
        cost_estimate=pl.CostEstimate(
            flops=4 * channels * nblocks * tap_count * tap_count,
            bytes_accessed=3 * late.size * 2 + fir_taps.size * 2,
            transcendentals=0,
        ),
    )(fir_taps, early, late)


def shards(strain, fir_taps):
    tap_count = fir_taps.shape[1]
    channels = strain.shape[0]
    previous = shifted(strain[:, -tap_count:], "tm", 1)
    early = jnp.concatenate([previous, strain[:, :-tap_count]], axis=1)
    early = early.reshape(channels, -1, tap_count)
    late = strain.reshape(channels, -1, tap_count)
    whitened = whiten(fir_taps, early, late).reshape(channels, -1)
    segments = whitened.reshape(channels * (whitened.shape[1] // SEG), SEG)
    parts = lax.axis_size("tm")
    table = make_table()
    bins = table.shape[2]
    table = jnp.asarray(
        table.reshape(SEG, 2, parts, bins // parts).transpose(0, 2, 1, 3).reshape(SEG, 2 * bins)
    )
    spectra = jnp.einsum(
        "xn,nq->qx", segments, table, preferred_element_type=jnp.float32
    ).astype(jnp.bfloat16)
    spectra = spectra.reshape(parts, spectra.shape[0] // parts, spectra.shape[1])
    own = lax.all_to_all(spectra, "tm", split_axis=0, concat_axis=0, tiled=True)
    pairs = bins // parts // 2
    shard = own.reshape(parts, 2, pairs, 2, channels, -1).transpose(2, 4, 3, 1, 0, 5)
    shard = shard.reshape(pairs, channels, -1)
    every = lax.all_gather(shard, "chan", axis=0)
    return cross_spectra(lhs_rows(shard), every)


def lhs_rows(shard):
    pairs, channels, lanes = shard.shape
    split = shard.reshape(pairs, channels, 2, 2, lanes // 4)
    parity = lax.broadcasted_iota(jnp.int32, split.shape, 2)
    zero = jnp.zeros_like(split)
    swapped = jnp.concatenate([split[:, :, :, 1:], -split[:, :, :, :1]], axis=3)
    rows = []
    for part in (split, swapped):
        for b in range(2):
            rows.append(jnp.where(parity == b, part, zero).reshape(pairs, channels, lanes))
    return jnp.stack(rows, axis=1).reshape(pairs, 4 * channels, lanes)


def cross_kernel(lhs_ref, every_ref, out_ref):
    sources, count, channels, lanes = every_ref.shape
    factor = 1.0 / (lanes // 4 * SEG)
    for t in range(count):
        rhs = every_ref[:, t].reshape(sources * channels, lanes)
        prod = lax.dot_general(
            lhs_ref[t], rhs, (((1,), (1,)), ((), ())), preferred_element_type=jnp.float32
        )
        prod = prod * factor
        for q in range(4):
            out_ref[q // 2, 2 * t + q % 2] = prod[q * channels:(q + 1) * channels]


def cross_spectra(lhs, every):
    sources, pairs, channels, lanes = every.shape
    step = 8 if pairs % 8 == 0 else pairs
    wide = sources * channels
    return pl.pallas_call(
        cross_kernel,
        out_shape=jax.ShapeDtypeStruct((2, 2 * pairs, channels, wide), jnp.float32),
        grid=(pairs // step,),
        in_specs=[
            pl.BlockSpec((step, 4 * channels, lanes), lambda g: (g, 0, 0)),
            pl.BlockSpec((sources, step, channels, lanes), lambda g: (0, g, 0, 0)),
        ],
        out_specs=pl.BlockSpec((2, 2 * step, channels, wide), lambda g: (0, g, 0, 0)),
        cost_estimate=pl.CostEstimate(
            flops=2 * pairs * 4 * channels * lanes * wide,
            bytes_accessed=lhs.size * 2 + every.size * 2 + 2 * 2 * pairs * channels * wide * 4,
            transcendentals=0,
        ),
    )(lhs, every)


def solution(mesh):
    placed = (P("chan", "tm"), P("chan", None))
    return jax.shard_map(
        shards, mesh=mesh, in_specs=placed, out_specs=P(None, "tm", "chan", None), check_vma=False
    )
```

```python
import math

import jax
import ml_dtypes
import numpy as np
import jax.numpy as jnp
from jax import lax
from jax.experimental import pallas as pl
from jax.experimental.pallas import tpu as pltpu
from jax.sharding import PartitionSpec as P

SEG = 512


def shifted(value, axis, by):
    size = lax.axis_size(axis)
    pairs = [(i, i + by) for i in range(size) if 0 <= i + by < size]
    return lax.ppermute(value, axis, pairs)


def make_table():
    sample_idx = np.arange(SEG, dtype=np.int32)
    bin_idx = np.arange(SEG // 2, dtype=np.int32)
    phases = sample_idx[:, None] * bin_idx[None, :] % SEG
    step = np.float32(2.0 * math.pi / SEG)
    angles = phases.astype(np.float32) * step
    window = np.float32(0.5) - np.float32(0.5) * np.cos(sample_idx.astype(np.float32) * step)
    cosine = window[:, None] * np.cos(angles)
    sine_part = -window[:, None] * np.sin(angles)
    return np.stack([cosine, sine_part], axis=1).astype(ml_dtypes.bfloat16)


def toeplitz(fir_taps):
    tap_count = fir_taps.shape[1]
    row_idx = jnp.arange(2 * tap_count, dtype=jnp.int32)[:, None]
    col_idx = jnp.arange(tap_count, dtype=jnp.int32)[None, :]
    lag_idx = col_idx + tap_count - row_idx
    valid = (lag_idx >= 0) & (lag_idx < tap_count)
    picked = jnp.take(fir_taps, jnp.clip(lag_idx, 0, tap_count - 1), axis=1)
    return jnp.where(valid[None, :, :], picked, jnp.zeros_like(picked))


def cross_block(own_bins, other_bins):
    swapped = jnp.stack([-other_bins[:, 1], other_bins[:, 0]], axis=1)
    real_part = jnp.einsum(
        "kpsi,kpsj->kij", own_bins, other_bins, preferred_element_type=jnp.float32
    )
    imag_part = jnp.einsum("kpsi,kpsj->kij", own_bins, swapped, preferred_element_type=jnp.float32)
    return jnp.stack([real_part, imag_part], axis=0)


def fir_kernel(taps_ref, previous_ref, late_ref, out_ref):
    half = taps_ref.shape[1] // 2
    row = lax.broadcasted_iota(jnp.int32, (half, half), 0)
    col = lax.broadcasted_iota(jnp.int32, (half, half), 1)
    upper = col >= row
    zero = jnp.zeros((half, half), jnp.float32)
    first = lax.broadcasted_iota(jnp.int32, late_ref.shape[1:], 0) == 0
    for ci in range(taps_ref.shape[0]):
        taps = taps_ref[pl.ds(ci, 1), :].astype(jnp.float32)
        low = jnp.broadcast_to(taps[:, :half], (half, half))
        high = jnp.broadcast_to(taps[:, half:], (half, half))
        low = pltpu.roll(low, 0, 1, stride=1, stride_axis=0)
        high = pltpu.roll(high, 0, 1, stride=1, stride_axis=0)
        d0 = jnp.where(upper, zero, high).astype(jnp.bfloat16)
        d1 = jnp.where(upper, high, low).astype(jnp.bfloat16)
        d2 = jnp.where(upper, low, zero).astype(jnp.bfloat16)
        none = jnp.zeros_like(d0)
        top = jnp.concatenate(
            [jnp.concatenate([d0, none], axis=1), jnp.concatenate([d1, d0], axis=1)], axis=0
        )
        bottom = jnp.concatenate(
            [jnp.concatenate([d2, d1], axis=1), jnp.concatenate([none, d2], axis=1)], axis=0
        )
        late = late_ref[ci]
        shifted_down = pltpu.roll(jnp.dot(late, top, preferred_element_type=jnp.float32), 1, 0)
        head = jnp.dot(previous_ref[pl.ds(ci, 1), :], top, preferred_element_type=jnp.float32)
        acc = jnp.where(first, jnp.broadcast_to(head, shifted_down.shape), shifted_down)
        acc = acc + jnp.dot(late, bottom, preferred_element_type=jnp.float32)
        out_ref[ci] = acc.astype(out_ref.dtype)


def whiten(fir_taps, previous, late):
    channels, nblocks, tap_count = late.shape
    group = 8
    block = pl.BlockSpec((group, nblocks, tap_count), lambda g: (g, 0, 0))
    rows = pl.BlockSpec((group, tap_count), lambda g: (g, 0))
    return pl.pallas_call(
        fir_kernel,
        out_shape=jax.ShapeDtypeStruct(late.shape, jnp.bfloat16),
        grid=(channels // group,),
        in_specs=[rows, rows, block],
        out_specs=block,
        cost_estimate=pl.CostEstimate(
            flops=4 * channels * nblocks * tap_count * tap_count,
            bytes_accessed=2 * late.size * 2 + 2 * fir_taps.size * 2,
            transcendentals=0,
        ),
    )(fir_taps, previous, late)


def shards(strain, fir_taps):
    tap_count = fir_taps.shape[1]
    channels = strain.shape[0]
    previous = shifted(strain[:, -tap_count:], "tm", 1)
    late = strain.reshape(channels, -1, tap_count)
    whitened = whiten(fir_taps, previous, late).reshape(channels, -1)
    segments = whitened.reshape(channels * (whitened.shape[1] // SEG), SEG)
    parts = lax.axis_size("tm")
    table = make_table()
    bins = table.shape[2]
    table = jnp.asarray(
        table.reshape(SEG, 2, parts, bins // parts).transpose(0, 2, 1, 3).reshape(SEG, 2 * bins)
    )
    spectra = jnp.einsum(
        "xn,nq->qx", segments, table, preferred_element_type=jnp.float32
    ).astype(jnp.bfloat16)
    spectra = spectra.reshape(parts, spectra.shape[0] // parts, spectra.shape[1])
    own = lax.all_to_all(spectra, "tm", split_axis=0, concat_axis=0, tiled=True)
    pairs = bins // parts // 2
    shard = own.reshape(parts, 2, pairs, 2, channels, -1).transpose(2, 4, 3, 1, 0, 5)
    shard = shard.reshape(pairs, channels, -1)
    every = lax.all_gather(shard, "chan", axis=0)
    return cross_spectra(lhs_rows(shard), every)


def lhs_rows(shard):
    pairs, channels, lanes = shard.shape
    split = shard.reshape(pairs, channels, 2, 2, lanes // 4)
    parity = lax.broadcasted_iota(jnp.int32, split.shape, 2)
    zero = jnp.zeros_like(split)
    swapped = jnp.concatenate([split[:, :, :, 1:], -split[:, :, :, :1]], axis=3)
    rows = []
    for part in (split, swapped):
        for b in range(2):
            rows.append(jnp.where(parity == b, part, zero).reshape(pairs, channels, lanes))
    return jnp.stack(rows, axis=1).reshape(pairs, 4 * channels, lanes)


def cross_kernel(lhs_ref, every_ref, out_ref):
    sources, count, channels, lanes = every_ref.shape
    factor = 1.0 / (lanes // 4 * SEG)
    for t in range(count):
        rhs = every_ref[:, t].reshape(sources * channels, lanes)
        prod = lax.dot_general(
            lhs_ref[t], rhs, (((1,), (1,)), ((), ())), preferred_element_type=jnp.float32
        )
        prod = prod * factor
        for q in range(4):
            out_ref[q // 2, 2 * t + q % 2] = prod[q * channels:(q + 1) * channels]


def cross_spectra(lhs, every):
    sources, pairs, channels, lanes = every.shape
    step = 8 if pairs % 8 == 0 else pairs
    wide = sources * channels
    return pl.pallas_call(
        cross_kernel,
        out_shape=jax.ShapeDtypeStruct((2, 2 * pairs, channels, wide), jnp.float32),
        grid=(pairs // step,),
        in_specs=[
            pl.BlockSpec((step, 4 * channels, lanes), lambda g: (g, 0, 0)),
            pl.BlockSpec((sources, step, channels, lanes), lambda g: (0, g, 0, 0)),
        ],
        out_specs=pl.BlockSpec((2, 2 * step, channels, wide), lambda g: (0, g, 0, 0)),
        cost_estimate=pl.CostEstimate(
            flops=2 * pairs * 4 * channels * lanes * wide,
            bytes_accessed=lhs.size * 2 + every.size * 2 + 2 * 2 * pairs * channels * wide * 4,
            transcendentals=0,
        ),
    )(lhs, every)


def solution(mesh):
    placed = (P("chan", "tm"), P("chan", None))
    return jax.shard_map(
        shards, mesh=mesh, in_specs=placed, out_specs=P(None, "tm", "chan", None), check_vma=False
    )
```

```python
import math

import jax
import ml_dtypes
import numpy as np
import jax.numpy as jnp
from jax import lax
from jax.experimental import pallas as pl
from jax.experimental.pallas import tpu as pltpu
from jax.sharding import PartitionSpec as P

SEG = 512


def shifted(value, axis, by):
    size = lax.axis_size(axis)
    pairs = [(i, i + by) for i in range(size) if 0 <= i + by < size]
    return lax.ppermute(value, axis, pairs)


def make_table():
    sample_idx = np.arange(SEG, dtype=np.int32)
    bin_idx = np.arange(SEG // 2, dtype=np.int32)
    phases = sample_idx[:, None] * bin_idx[None, :] % SEG
    step = np.float32(2.0 * math.pi / SEG)
    angles = phases.astype(np.float32) * step
    window = np.float32(0.5) - np.float32(0.5) * np.cos(sample_idx.astype(np.float32) * step)
    cosine = window[:, None] * np.cos(angles)
    sine_part = -window[:, None] * np.sin(angles)
    return np.stack([cosine, sine_part], axis=1).astype(ml_dtypes.bfloat16)


def toeplitz(fir_taps):
    tap_count = fir_taps.shape[1]
    row_idx = jnp.arange(2 * tap_count, dtype=jnp.int32)[:, None]
    col_idx = jnp.arange(tap_count, dtype=jnp.int32)[None, :]
    lag_idx = col_idx + tap_count - row_idx
    valid = (lag_idx >= 0) & (lag_idx < tap_count)
    picked = jnp.take(fir_taps, jnp.clip(lag_idx, 0, tap_count - 1), axis=1)
    return jnp.where(valid[None, :, :], picked, jnp.zeros_like(picked))


def cross_block(own_bins, other_bins):
    swapped = jnp.stack([-other_bins[:, 1], other_bins[:, 0]], axis=1)
    real_part = jnp.einsum(
        "kpsi,kpsj->kij", own_bins, other_bins, preferred_element_type=jnp.float32
    )
    imag_part = jnp.einsum("kpsi,kpsj->kij", own_bins, swapped, preferred_element_type=jnp.float32)
    return jnp.stack([real_part, imag_part], axis=0)


def fir_kernel(taps_ref, previous_ref, late_ref, out_ref):
    half = taps_ref.shape[1] // 2
    row = lax.broadcasted_iota(jnp.int32, (half, half), 0)
    col = lax.broadcasted_iota(jnp.int32, (half, half), 1)
    upper = col >= row
    zero = jnp.zeros((half, half), jnp.float32)
    first = lax.broadcasted_iota(jnp.int32, late_ref.shape[1:], 0) == 0
    for ci in range(taps_ref.shape[0]):
        taps = taps_ref[pl.ds(ci, 1), :].astype(jnp.float32)
        low = jnp.broadcast_to(taps[:, :half], (half, half))
        high = jnp.broadcast_to(taps[:, half:], (half, half))
        low = pltpu.roll(low, 0, 1, stride=1, stride_axis=0)
        high = pltpu.roll(high, 0, 1, stride=1, stride_axis=0)
        d0 = jnp.where(upper, zero, high).astype(jnp.bfloat16)
        d1 = jnp.where(upper, high, low).astype(jnp.bfloat16)
        d2 = jnp.where(upper, low, zero).astype(jnp.bfloat16)
        none = jnp.zeros_like(d0)
        top = jnp.concatenate(
            [jnp.concatenate([d0, none], axis=1), jnp.concatenate([d1, d0], axis=1)], axis=0
        )
        bottom = jnp.concatenate(
            [jnp.concatenate([d2, d1], axis=1), jnp.concatenate([none, d2], axis=1)], axis=0
        )
        late = late_ref[ci]
        shifted_down = pltpu.roll(jnp.dot(late, top, preferred_element_type=jnp.float32), 1, 0)
        head = jnp.dot(previous_ref[pl.ds(ci, 1), :], top, preferred_element_type=jnp.float32)
        acc = jnp.where(first, jnp.broadcast_to(head, shifted_down.shape), shifted_down)
        acc = acc + jnp.dot(late, bottom, preferred_element_type=jnp.float32)
        out_ref[ci] = acc.astype(out_ref.dtype)


def whiten(fir_taps, previous, late):
    channels, nblocks, tap_count = late.shape
    group = 8
    block = pl.BlockSpec((group, nblocks, tap_count), lambda g: (g, 0, 0))
    rows = pl.BlockSpec((group, tap_count), lambda g: (g, 0))
    return pl.pallas_call(
        fir_kernel,
        out_shape=jax.ShapeDtypeStruct(late.shape, jnp.bfloat16),
        grid=(channels // group,),
        in_specs=[rows, rows, block],
        out_specs=block,
        cost_estimate=pl.CostEstimate(
            flops=4 * channels * nblocks * tap_count * tap_count,
            bytes_accessed=2 * late.size * 2 + 2 * fir_taps.size * 2,
            transcendentals=0,
        ),
    )(fir_taps, previous, late)


def shards(strain, fir_taps):
    tap_count = fir_taps.shape[1]
    channels = strain.shape[0]
    previous = shifted(strain[:, -tap_count:], "tm", 1)
    late = strain.reshape(channels, -1, tap_count)
    whitened = whiten(fir_taps, previous, late).reshape(channels, -1)
    segments = whitened.reshape(channels * (whitened.shape[1] // SEG), SEG)
    parts = lax.axis_size("tm")
    table = make_table()
    bins = table.shape[2]
    table = jnp.asarray(
        table.reshape(SEG, 2, parts, bins // parts).transpose(0, 2, 1, 3).reshape(SEG, 2 * bins)
    )
    spectra = jnp.einsum(
        "xn,nq->qx", segments, table, preferred_element_type=jnp.float32
    ).astype(jnp.bfloat16)
    spectra = spectra.reshape(parts, spectra.shape[0] // parts, spectra.shape[1])
    own = lax.all_to_all(spectra, "tm", split_axis=0, concat_axis=0, tiled=True)
    pairs = bins // parts // 2
    shard = own.reshape(parts, 2, pairs, 2, channels, -1).transpose(2, 4, 3, 1, 0, 5)
    shard = shard.reshape(pairs, channels, -1)
    every = lax.all_gather(shard, "chan", axis=0)
    return cross_spectra(lhs_rows(shard), every)


def lhs_rows(shard):
    pairs, channels, lanes = shard.shape
    split = shard.reshape(pairs, channels, 2, 2, lanes // 4)
    parity = lax.broadcasted_iota(jnp.int32, split.shape, 2)
    zero = jnp.zeros_like(split)
    swapped = jnp.concatenate([split[:, :, :, 1:], -split[:, :, :, :1]], axis=3)
    rows = []
    for part in (split, swapped):
        for b in range(2):
            rows.append(jnp.where(parity == b, part, zero).reshape(pairs, channels, lanes))
    return jnp.stack(rows, axis=1).reshape(pairs, 4 * channels, lanes)


def cross_kernel(lhs_ref, every_ref, out_ref):
    sources, count, channels, lanes = every_ref.shape
    factor = 1.0 / (lanes // 4 * SEG)
    for t in range(count):
        rhs = every_ref[:, t].reshape(sources * channels, lanes)
        prod = lax.dot_general(
            lhs_ref[t], rhs, (((1,), (1,)), ((), ())), preferred_element_type=jnp.float32
        )
        prod = prod * factor
        for q in range(4):
            out_ref[q // 2, 2 * t + q % 2] = prod[q * channels:(q + 1) * channels]


def cross_spectra(lhs, every):
    sources, pairs, channels, lanes = every.shape
    step = 4 if pairs % 4 == 0 else pairs
    wide = sources * channels
    return pl.pallas_call(
        cross_kernel,
        out_shape=jax.ShapeDtypeStruct((2, 2 * pairs, channels, wide), jnp.float32),
        grid=(pairs // step,),
        in_specs=[
            pl.BlockSpec((step, 4 * channels, lanes), lambda g: (g, 0, 0)),
            pl.BlockSpec((sources, step, channels, lanes), lambda g: (0, g, 0, 0)),
        ],
        out_specs=pl.BlockSpec((2, 2 * step, channels, wide), lambda g: (0, g, 0, 0)),
        cost_estimate=pl.CostEstimate(
            flops=2 * pairs * 4 * channels * lanes * wide,
            bytes_accessed=lhs.size * 2 + every.size * 2 + 2 * 2 * pairs * channels * wide * 4,
            transcendentals=0,
        ),
    )(lhs, every)


def solution(mesh):
    placed = (P("chan", "tm"), P("chan", None))
    return jax.shard_map(
        shards, mesh=mesh, in_specs=placed, out_specs=P(None, "tm", "chan", None), check_vma=False
    )
```

```python
import math

import jax
import ml_dtypes
import numpy as np
import jax.numpy as jnp
from jax import lax
from jax.experimental import pallas as pl
from jax.experimental.pallas import tpu as pltpu
from jax.sharding import PartitionSpec as P

SEG = 512


def shifted(value, axis, by):
    size = lax.axis_size(axis)
    pairs = [(i, i + by) for i in range(size) if 0 <= i + by < size]
    return lax.ppermute(value, axis, pairs)


def make_table():
    sample_idx = np.arange(SEG, dtype=np.int32)
    bin_idx = np.arange(SEG // 2, dtype=np.int32)
    phases = sample_idx[:, None] * bin_idx[None, :] % SEG
    step = np.float32(2.0 * math.pi / SEG)
    angles = phases.astype(np.float32) * step
    window = np.float32(0.5) - np.float32(0.5) * np.cos(sample_idx.astype(np.float32) * step)
    cosine = window[:, None] * np.cos(angles)
    sine_part = -window[:, None] * np.sin(angles)
    return np.stack([cosine, sine_part], axis=1).astype(ml_dtypes.bfloat16)


def toeplitz(fir_taps):
    tap_count = fir_taps.shape[1]
    row_idx = jnp.arange(2 * tap_count, dtype=jnp.int32)[:, None]
    col_idx = jnp.arange(tap_count, dtype=jnp.int32)[None, :]
    lag_idx = col_idx + tap_count - row_idx
    valid = (lag_idx >= 0) & (lag_idx < tap_count)
    picked = jnp.take(fir_taps, jnp.clip(lag_idx, 0, tap_count - 1), axis=1)
    return jnp.where(valid[None, :, :], picked, jnp.zeros_like(picked))


def cross_block(own_bins, other_bins):
    swapped = jnp.stack([-other_bins[:, 1], other_bins[:, 0]], axis=1)
    real_part = jnp.einsum(
        "kpsi,kpsj->kij", own_bins, other_bins, preferred_element_type=jnp.float32
    )
    imag_part = jnp.einsum("kpsi,kpsj->kij", own_bins, swapped, preferred_element_type=jnp.float32)
    return jnp.stack([real_part, imag_part], axis=0)


def fir_kernel(taps_ref, previous_ref, late_ref, out_ref):
    half = taps_ref.shape[1] // 2
    row = lax.broadcasted_iota(jnp.int32, (half, half), 0)
    col = lax.broadcasted_iota(jnp.int32, (half, half), 1)
    upper = col >= row
    zero = jnp.zeros((half, half), jnp.float32)
    first = lax.broadcasted_iota(jnp.int32, late_ref.shape[1:], 0) == 0
    for ci in range(taps_ref.shape[0]):
        taps = taps_ref[pl.ds(ci, 1), :].astype(jnp.float32)
        low = jnp.broadcast_to(taps[:, :half], (half, half))
        high = jnp.broadcast_to(taps[:, half:], (half, half))
        low = pltpu.roll(low, 0, 1, stride=1, stride_axis=0)
        high = pltpu.roll(high, 0, 1, stride=1, stride_axis=0)
        d0 = jnp.where(upper, zero, high).astype(jnp.bfloat16)
        d1 = jnp.where(upper, high, low).astype(jnp.bfloat16)
        d2 = jnp.where(upper, low, zero).astype(jnp.bfloat16)
        none = jnp.zeros_like(d0)
        top = jnp.concatenate(
            [jnp.concatenate([d0, none], axis=1), jnp.concatenate([d1, d0], axis=1)], axis=0
        )
        bottom = jnp.concatenate(
            [jnp.concatenate([d2, d1], axis=1), jnp.concatenate([none, d2], axis=1)], axis=0
        )
        late = late_ref[ci]
        shifted_down = pltpu.roll(jnp.dot(late, top, preferred_element_type=jnp.float32), 1, 0)
        head = jnp.dot(previous_ref[pl.ds(ci, 1), :], top, preferred_element_type=jnp.float32)
        acc = jnp.where(first, jnp.broadcast_to(head, shifted_down.shape), shifted_down)
        acc = acc + jnp.dot(late, bottom, preferred_element_type=jnp.float32)
        out_ref[ci] = acc.astype(out_ref.dtype)


def whiten(fir_taps, previous, late):
    channels, nblocks, tap_count = late.shape
    group = 8
    block = pl.BlockSpec((group, nblocks, tap_count), lambda g: (g, 0, 0))
    rows = pl.BlockSpec((group, tap_count), lambda g: (g, 0))
    return pl.pallas_call(
        fir_kernel,
        out_shape=jax.ShapeDtypeStruct(late.shape, jnp.bfloat16),
        grid=(channels // group,),
        in_specs=[rows, rows, block],
        out_specs=block,
        cost_estimate=pl.CostEstimate(
            flops=4 * channels * nblocks * tap_count * tap_count,
            bytes_accessed=2 * late.size * 2 + 2 * fir_taps.size * 2,
            transcendentals=0,
        ),
    )(fir_taps, previous, late)


def shards(strain, fir_taps):
    tap_count = fir_taps.shape[1]
    channels = strain.shape[0]
    previous = shifted(strain[:, -tap_count:], "tm", 1)
    late = strain.reshape(channels, -1, tap_count)
    whitened = whiten(fir_taps, previous, late).reshape(channels, -1)
    segments = whitened.reshape(channels * (whitened.shape[1] // SEG), SEG)
    parts = lax.axis_size("tm")
    table = make_table()
    bins = table.shape[2]
    table = jnp.asarray(
        table.reshape(SEG, 2, parts, bins // parts).transpose(0, 2, 1, 3).reshape(SEG, 2 * bins)
    )
    spectra = jnp.einsum(
        "xn,nq->qx", segments, table, preferred_element_type=jnp.float32
    ).astype(jnp.bfloat16)
    spectra = spectra.reshape(parts, spectra.shape[0] // parts, spectra.shape[1])
    own = lax.all_to_all(spectra, "tm", split_axis=0, concat_axis=0, tiled=True)
    pairs = bins // parts // 2
    shard = own.reshape(parts, 2, pairs, 2, channels, -1).transpose(2, 4, 3, 1, 0, 5)
    shard = shard.reshape(pairs, channels, -1)
    every = lax.all_gather(shard, "chan", axis=0)
    return cross_spectra(lhs_rows(shard), every)


def lhs_rows(shard):
    pairs, channels, lanes = shard.shape
    split = shard.reshape(pairs, channels, 2, 2, lanes // 4)
    parity = lax.broadcasted_iota(jnp.int32, split.shape, 2)
    zero = jnp.zeros_like(split)
    swapped = jnp.concatenate([split[:, :, :, 1:], -split[:, :, :, :1]], axis=3)
    rows = []
    for part in (split, swapped):
        for b in range(2):
            rows.append(jnp.where(parity == b, part, zero).reshape(pairs, channels, lanes))
    return jnp.stack(rows, axis=1).reshape(pairs, 4 * channels, lanes)


def cross_kernel(lhs_ref, every_ref, out_ref):
    sources, count, channels, lanes = every_ref.shape
    factor = 1.0 / (lanes // 4 * SEG)
    for t in range(count):
        rhs = every_ref[:, t].reshape(sources * channels, lanes)
        prod = lax.dot_general(
            lhs_ref[t], rhs, (((1,), (1,)), ((), ())), preferred_element_type=jnp.float32
        )
        prod = prod * factor
        for q in range(4):
            out_ref[q // 2, 2 * t + q % 2] = prod[q * channels:(q + 1) * channels]


def cross_spectra(lhs, every):
    sources, pairs, channels, lanes = every.shape
    step = 16 if pairs % 16 == 0 else pairs
    wide = sources * channels
    return pl.pallas_call(
        cross_kernel,
        out_shape=jax.ShapeDtypeStruct((2, 2 * pairs, channels, wide), jnp.float32),
        grid=(pairs // step,),
        in_specs=[
            pl.BlockSpec((step, 4 * channels, lanes), lambda g: (g, 0, 0)),
            pl.BlockSpec((sources, step, channels, lanes), lambda g: (0, g, 0, 0)),
        ],
        out_specs=pl.BlockSpec((2, 2 * step, channels, wide), lambda g: (0, g, 0, 0)),
        cost_estimate=pl.CostEstimate(
            flops=2 * pairs * 4 * channels * lanes * wide,
            bytes_accessed=lhs.size * 2 + every.size * 2 + 2 * 2 * pairs * channels * wide * 4,
            transcendentals=0,
        ),
    )(lhs, every)


def solution(mesh):
    placed = (P("chan", "tm"), P("chan", None))
    return jax.shard_map(
        shards, mesh=mesh, in_specs=placed, out_specs=P(None, "tm", "chan", None), check_vma=False
    )
```

```python
import math

import jax
import ml_dtypes
import numpy as np
import jax.numpy as jnp
from jax import lax
from jax.experimental import pallas as pl
from jax.experimental.pallas import tpu as pltpu
from jax.sharding import PartitionSpec as P

SEG = 512


def shifted(value, axis, by):
    size = lax.axis_size(axis)
    pairs = [(i, i + by) for i in range(size) if 0 <= i + by < size]
    return lax.ppermute(value, axis, pairs)


def make_table():
    sample_idx = np.arange(SEG, dtype=np.int32)
    bin_idx = np.arange(SEG // 2, dtype=np.int32)
    phases = sample_idx[:, None] * bin_idx[None, :] % SEG
    step = np.float32(2.0 * math.pi / SEG)
    angles = phases.astype(np.float32) * step
    window = np.float32(0.5) - np.float32(0.5) * np.cos(sample_idx.astype(np.float32) * step)
    cosine = window[:, None] * np.cos(angles)
    sine_part = -window[:, None] * np.sin(angles)
    return np.stack([cosine, sine_part], axis=1).astype(ml_dtypes.bfloat16)


def toeplitz(fir_taps):
    tap_count = fir_taps.shape[1]
    row_idx = jnp.arange(2 * tap_count, dtype=jnp.int32)[:, None]
    col_idx = jnp.arange(tap_count, dtype=jnp.int32)[None, :]
    lag_idx = col_idx + tap_count - row_idx
    valid = (lag_idx >= 0) & (lag_idx < tap_count)
    picked = jnp.take(fir_taps, jnp.clip(lag_idx, 0, tap_count - 1), axis=1)
    return jnp.where(valid[None, :, :], picked, jnp.zeros_like(picked))


def cross_block(own_bins, other_bins):
    swapped = jnp.stack([-other_bins[:, 1], other_bins[:, 0]], axis=1)
    real_part = jnp.einsum(
        "kpsi,kpsj->kij", own_bins, other_bins, preferred_element_type=jnp.float32
    )
    imag_part = jnp.einsum("kpsi,kpsj->kij", own_bins, swapped, preferred_element_type=jnp.float32)
    return jnp.stack([real_part, imag_part], axis=0)


def fir_kernel(taps_ref, previous_ref, late_ref, out_ref):
    half = taps_ref.shape[1] // 2
    row = lax.broadcasted_iota(jnp.int32, (half, half), 0)
    col = lax.broadcasted_iota(jnp.int32, (half, half), 1)
    upper = col >= row
    zero = jnp.zeros((half, half), jnp.float32)
    first = lax.broadcasted_iota(jnp.int32, late_ref.shape[1:], 0) == 0
    for ci in range(taps_ref.shape[0]):
        taps = taps_ref[pl.ds(ci, 1), :].astype(jnp.float32)
        low = jnp.broadcast_to(taps[:, :half], (half, half))
        high = jnp.broadcast_to(taps[:, half:], (half, half))
        low = pltpu.roll(low, 0, 1, stride=1, stride_axis=0)
        high = pltpu.roll(high, 0, 1, stride=1, stride_axis=0)
        d0 = jnp.where(upper, zero, high).astype(jnp.bfloat16)
        d1 = jnp.where(upper, high, low).astype(jnp.bfloat16)
        d2 = jnp.where(upper, low, zero).astype(jnp.bfloat16)
        none = jnp.zeros_like(d0)
        top = jnp.concatenate(
            [jnp.concatenate([d0, none], axis=1), jnp.concatenate([d1, d0], axis=1)], axis=0
        )
        bottom = jnp.concatenate(
            [jnp.concatenate([d2, d1], axis=1), jnp.concatenate([none, d2], axis=1)], axis=0
        )
        late = late_ref[ci]
        shifted_down = pltpu.roll(jnp.dot(late, top, preferred_element_type=jnp.float32), 1, 0)
        head = jnp.dot(previous_ref[pl.ds(ci, 1), :], top, preferred_element_type=jnp.float32)
        acc = jnp.where(first, jnp.broadcast_to(head, shifted_down.shape), shifted_down)
        acc = acc + jnp.dot(late, bottom, preferred_element_type=jnp.float32)
        out_ref[ci] = acc.astype(out_ref.dtype)


def whiten(fir_taps, previous, late):
    channels, nblocks, tap_count = late.shape
    group = 16 if channels % 16 == 0 else channels
    block = pl.BlockSpec((group, nblocks, tap_count), lambda g: (g, 0, 0))
    rows = pl.BlockSpec((group, tap_count), lambda g: (g, 0))
    return pl.pallas_call(
        fir_kernel,
        out_shape=jax.ShapeDtypeStruct(late.shape, jnp.bfloat16),
        grid=(channels // group,),
        in_specs=[rows, rows, block],
        out_specs=block,
        cost_estimate=pl.CostEstimate(
            flops=4 * channels * nblocks * tap_count * tap_count,
            bytes_accessed=2 * late.size * 2 + 2 * fir_taps.size * 2,
            transcendentals=0,
        ),
    )(fir_taps, previous, late)


def shards(strain, fir_taps):
    tap_count = fir_taps.shape[1]
    channels = strain.shape[0]
    previous = shifted(strain[:, -tap_count:], "tm", 1)
    late = strain.reshape(channels, -1, tap_count)
    whitened = whiten(fir_taps, previous, late).reshape(channels, -1)
    segments = whitened.reshape(channels * (whitened.shape[1] // SEG), SEG)
    parts = lax.axis_size("tm")
    table = make_table()
    bins = table.shape[2]
    table = jnp.asarray(
        table.reshape(SEG, 2, parts, bins // parts).transpose(0, 2, 1, 3).reshape(SEG, 2 * bins)
    )
    spectra = jnp.einsum(
        "xn,nq->qx", segments, table, preferred_element_type=jnp.float32
    ).astype(jnp.bfloat16)
    spectra = spectra.reshape(parts, spectra.shape[0] // parts, spectra.shape[1])
    own = lax.all_to_all(spectra, "tm", split_axis=0, concat_axis=0, tiled=True)
    pairs = bins // parts // 2
    shard = own.reshape(parts, 2, pairs, 2, channels, -1).transpose(2, 4, 3, 1, 0, 5)
    shard = shard.reshape(pairs, channels, -1)
    every = lax.all_gather(shard, "chan", axis=0)
    return cross_spectra(lhs_rows(shard), every)


def lhs_rows(shard):
    pairs, channels, lanes = shard.shape
    split = shard.reshape(pairs, channels, 2, 2, lanes // 4)
    parity = lax.broadcasted_iota(jnp.int32, split.shape, 2)
    zero = jnp.zeros_like(split)
    swapped = jnp.concatenate([split[:, :, :, 1:], -split[:, :, :, :1]], axis=3)
    rows = []
    for part in (split, swapped):
        for b in range(2):
            rows.append(jnp.where(parity == b, part, zero).reshape(pairs, channels, lanes))
    return jnp.stack(rows, axis=1).reshape(pairs, 4 * channels, lanes)


def cross_kernel(lhs_ref, every_ref, out_ref):
    sources, count, channels, lanes = every_ref.shape
    factor = 1.0 / (lanes // 4 * SEG)
    for t in range(count):
        rhs = every_ref[:, t].reshape(sources * channels, lanes)
        prod = lax.dot_general(
            lhs_ref[t], rhs, (((1,), (1,)), ((), ())), preferred_element_type=jnp.float32
        )
        prod = prod * factor
        for q in range(4):
            out_ref[q // 2, 2 * t + q % 2] = prod[q * channels:(q + 1) * channels]


def cross_spectra(lhs, every):
    sources, pairs, channels, lanes = every.shape
    step = 16 if pairs % 16 == 0 else pairs
    wide = sources * channels
    return pl.pallas_call(
        cross_kernel,
        out_shape=jax.ShapeDtypeStruct((2, 2 * pairs, channels, wide), jnp.float32),
        grid=(pairs // step,),
        in_specs=[
            pl.BlockSpec((step, 4 * channels, lanes), lambda g: (g, 0, 0)),
            pl.BlockSpec((sources, step, channels, lanes), lambda g: (0, g, 0, 0)),
        ],
        out_specs=pl.BlockSpec((2, 2 * step, channels, wide), lambda g: (0, g, 0, 0)),
        cost_estimate=pl.CostEstimate(
            flops=2 * pairs * 4 * channels * lanes * wide,
            bytes_accessed=lhs.size * 2 + every.size * 2 + 2 * 2 * pairs * channels * wide * 4,
            transcendentals=0,
        ),
    )(lhs, every)


def solution(mesh):
    placed = (P("chan", "tm"), P("chan", None))
    return jax.shard_map(
        shards, mesh=mesh, in_specs=placed, out_specs=P(None, "tm", "chan", None), check_vma=False
    )
```

```python
import math

import jax
import ml_dtypes
import numpy as np
import jax.numpy as jnp
from jax import lax
from jax.experimental import pallas as pl
from jax.experimental.pallas import tpu as pltpu
from jax.sharding import PartitionSpec as P

SEG = 512


def shifted(value, axis, by):
    size = lax.axis_size(axis)
    pairs = [(i, i + by) for i in range(size) if 0 <= i + by < size]
    return lax.ppermute(value, axis, pairs)


def make_table():
    sample_idx = np.arange(SEG, dtype=np.int32)
    bin_idx = np.arange(SEG // 2, dtype=np.int32)
    phases = sample_idx[:, None] * bin_idx[None, :] % SEG
    step = np.float32(2.0 * math.pi / SEG)
    angles = phases.astype(np.float32) * step
    window = np.float32(0.5) - np.float32(0.5) * np.cos(sample_idx.astype(np.float32) * step)
    cosine = window[:, None] * np.cos(angles)
    sine_part = -window[:, None] * np.sin(angles)
    return np.stack([cosine, sine_part], axis=1).astype(ml_dtypes.bfloat16)


def toeplitz(fir_taps):
    tap_count = fir_taps.shape[1]
    row_idx = jnp.arange(2 * tap_count, dtype=jnp.int32)[:, None]
    col_idx = jnp.arange(tap_count, dtype=jnp.int32)[None, :]
    lag_idx = col_idx + tap_count - row_idx
    valid = (lag_idx >= 0) & (lag_idx < tap_count)
    picked = jnp.take(fir_taps, jnp.clip(lag_idx, 0, tap_count - 1), axis=1)
    return jnp.where(valid[None, :, :], picked, jnp.zeros_like(picked))


def cross_block(own_bins, other_bins):
    swapped = jnp.stack([-other_bins[:, 1], other_bins[:, 0]], axis=1)
    real_part = jnp.einsum(
        "kpsi,kpsj->kij", own_bins, other_bins, preferred_element_type=jnp.float32
    )
    imag_part = jnp.einsum("kpsi,kpsj->kij", own_bins, swapped, preferred_element_type=jnp.float32)
    return jnp.stack([real_part, imag_part], axis=0)


def fir_kernel(taps_ref, previous_ref, late_ref, out_ref):
    half = taps_ref.shape[1] // 2
    row = lax.broadcasted_iota(jnp.int32, (half, half), 0)
    col = lax.broadcasted_iota(jnp.int32, (half, half), 1)
    upper = col >= row
    zero = jnp.zeros((half, half), jnp.float32)
    first = lax.broadcasted_iota(jnp.int32, late_ref.shape[1:], 0) == 0
    for ci in range(taps_ref.shape[0]):
        taps = taps_ref[pl.ds(ci, 1), :].astype(jnp.float32)
        low = jnp.broadcast_to(taps[:, :half], (half, half))
        high = jnp.broadcast_to(taps[:, half:], (half, half))
        low = pltpu.roll(low, 0, 1, stride=1, stride_axis=0)
        high = pltpu.roll(high, 0, 1, stride=1, stride_axis=0)
        d0 = jnp.where(upper, zero, high).astype(jnp.bfloat16)
        d1 = jnp.where(upper, high, low).astype(jnp.bfloat16)
        d2 = jnp.where(upper, low, zero).astype(jnp.bfloat16)
        none = jnp.zeros_like(d0)
        top = jnp.concatenate(
            [jnp.concatenate([d0, none], axis=1), jnp.concatenate([d1, d0], axis=1)], axis=0
        )
        bottom = jnp.concatenate(
            [jnp.concatenate([d2, d1], axis=1), jnp.concatenate([none, d2], axis=1)], axis=0
        )
        late = late_ref[ci]
        shifted_down = pltpu.roll(jnp.dot(late, top, preferred_element_type=jnp.float32), 1, 0)
        head = jnp.dot(previous_ref[pl.ds(ci, 1), :], top, preferred_element_type=jnp.float32)
        acc = jnp.where(first, jnp.broadcast_to(head, shifted_down.shape), shifted_down)
        acc = acc + jnp.dot(late, bottom, preferred_element_type=jnp.float32)
        out_ref[ci] = acc.astype(out_ref.dtype)


def whiten(fir_taps, previous, late):
    channels, nblocks, tap_count = late.shape
    group = 16 if channels % 16 == 0 else channels
    block = pl.BlockSpec((group, nblocks, tap_count), lambda g: (g, 0, 0))
    rows = pl.BlockSpec((group, tap_count), lambda g: (g, 0))
    return pl.pallas_call(
        fir_kernel,
        out_shape=jax.ShapeDtypeStruct(late.shape, jnp.bfloat16),
        grid=(channels // group,),
        in_specs=[rows, rows, block],
        out_specs=block,
        cost_estimate=pl.CostEstimate(
            flops=4 * channels * nblocks * tap_count * tap_count,
            bytes_accessed=2 * late.size * 2 + 2 * fir_taps.size * 2,
            transcendentals=0,
        ),
    )(fir_taps, previous, late)


def shards(strain, fir_taps):
    tap_count = fir_taps.shape[1]
    channels = strain.shape[0]
    previous = shifted(strain[:, -tap_count:], "tm", 1)
    late = strain.reshape(channels, -1, tap_count)
    whitened = whiten(fir_taps, previous, late).reshape(channels, -1)
    segments = whitened.reshape(channels * (whitened.shape[1] // SEG), SEG)
    parts = lax.axis_size("tm")
    table = make_table()
    bins = table.shape[2]
    table = jnp.asarray(
        table.reshape(SEG, 2, parts, bins // parts).transpose(0, 2, 1, 3).reshape(SEG, 2 * bins)
    )
    spectra = jnp.einsum(
        "xn,nq->qx", segments, table, preferred_element_type=jnp.float32
    ).astype(jnp.bfloat16)
    spectra = spectra.reshape(parts, spectra.shape[0] // parts, spectra.shape[1])
    own = lax.all_to_all(spectra, "tm", split_axis=0, concat_axis=0, tiled=True)
    pairs = bins // parts // 2
    rows = own.reshape(parts, 2, pairs, 2, own.shape[-1]).transpose(2, 3, 1, 0, 4)
    segs = own.shape[-1] // channels
    shard = rows.reshape(pairs, 4 * parts, channels, segs).transpose(0, 2, 1, 3)
    shard = shard.reshape(pairs, channels, -1)
    every = lax.all_gather(shard, "chan", axis=0)
    return cross_spectra(lhs_rows(shard), every)


def lhs_rows(shard):
    pairs, channels, lanes = shard.shape
    split = shard.reshape(pairs, channels, 2, 2, lanes // 4)
    parity = lax.broadcasted_iota(jnp.int32, split.shape, 2)
    zero = jnp.zeros_like(split)
    swapped = jnp.concatenate([split[:, :, :, 1:], -split[:, :, :, :1]], axis=3)
    rows = []
    for part in (split, swapped):
        for b in range(2):
            rows.append(jnp.where(parity == b, part, zero).reshape(pairs, channels, lanes))
    return jnp.stack(rows, axis=1).reshape(pairs, 4 * channels, lanes)


def cross_kernel(lhs_ref, every_ref, out_ref):
    sources, count, channels, lanes = every_ref.shape
    factor = 1.0 / (lanes // 4 * SEG)
    for t in range(count):
        rhs = every_ref[:, t].reshape(sources * channels, lanes)
        prod = lax.dot_general(
            lhs_ref[t], rhs, (((1,), (1,)), ((), ())), preferred_element_type=jnp.float32
        )
        prod = prod * factor
        for q in range(4):
            out_ref[q // 2, 2 * t + q % 2] = prod[q * channels:(q + 1) * channels]


def cross_spectra(lhs, every):
    sources, pairs, channels, lanes = every.shape
    step = 16 if pairs % 16 == 0 else pairs
    wide = sources * channels
    return pl.pallas_call(
        cross_kernel,
        out_shape=jax.ShapeDtypeStruct((2, 2 * pairs, channels, wide), jnp.float32),
        grid=(pairs // step,),
        in_specs=[
            pl.BlockSpec((step, 4 * channels, lanes), lambda g: (g, 0, 0)),
            pl.BlockSpec((sources, step, channels, lanes), lambda g: (0, g, 0, 0)),
        ],
        out_specs=pl.BlockSpec((2, 2 * step, channels, wide), lambda g: (0, g, 0, 0)),
        cost_estimate=pl.CostEstimate(
            flops=2 * pairs * 4 * channels * lanes * wide,
            bytes_accessed=lhs.size * 2 + every.size * 2 + 2 * 2 * pairs * channels * wide * 4,
            transcendentals=0,
        ),
    )(lhs, every)


def solution(mesh):
    placed = (P("chan", "tm"), P("chan", None))
    return jax.shard_map(
        shards, mesh=mesh, in_specs=placed, out_specs=P(None, "tm", "chan", None), check_vma=False
    )
```

```python
import math

import jax
import ml_dtypes
import numpy as np
import jax.numpy as jnp
from jax import lax
from jax.experimental import pallas as pl
from jax.experimental.pallas import tpu as pltpu
from jax.sharding import PartitionSpec as P

SEG = 512


def shifted(value, axis, by):
    size = lax.axis_size(axis)
    pairs = [(i, i + by) for i in range(size) if 0 <= i + by < size]
    return lax.ppermute(value, axis, pairs)


def make_table():
    sample_idx = np.arange(SEG, dtype=np.int32)
    bin_idx = np.arange(SEG // 2, dtype=np.int32)
    phases = sample_idx[:, None] * bin_idx[None, :] % SEG
    step = np.float32(2.0 * math.pi / SEG)
    angles = phases.astype(np.float32) * step
    window = np.float32(0.5) - np.float32(0.5) * np.cos(sample_idx.astype(np.float32) * step)
    cosine = window[:, None] * np.cos(angles)
    sine_part = -window[:, None] * np.sin(angles)
    return np.stack([cosine, sine_part], axis=1).astype(ml_dtypes.bfloat16)


def toeplitz(fir_taps):
    tap_count = fir_taps.shape[1]
    row_idx = jnp.arange(2 * tap_count, dtype=jnp.int32)[:, None]
    col_idx = jnp.arange(tap_count, dtype=jnp.int32)[None, :]
    lag_idx = col_idx + tap_count - row_idx
    valid = (lag_idx >= 0) & (lag_idx < tap_count)
    picked = jnp.take(fir_taps, jnp.clip(lag_idx, 0, tap_count - 1), axis=1)
    return jnp.where(valid[None, :, :], picked, jnp.zeros_like(picked))


def cross_block(own_bins, other_bins):
    swapped = jnp.stack([-other_bins[:, 1], other_bins[:, 0]], axis=1)
    real_part = jnp.einsum(
        "kpsi,kpsj->kij", own_bins, other_bins, preferred_element_type=jnp.float32
    )
    imag_part = jnp.einsum("kpsi,kpsj->kij", own_bins, swapped, preferred_element_type=jnp.float32)
    return jnp.stack([real_part, imag_part], axis=0)


def fir_kernel(taps_ref, previous_ref, late_ref, out_ref):
    half = taps_ref.shape[1] // 2
    row = lax.broadcasted_iota(jnp.int32, (half, half), 0)
    col = lax.broadcasted_iota(jnp.int32, (half, half), 1)
    upper = col >= row
    zero = jnp.zeros((half, half), jnp.float32)
    first = lax.broadcasted_iota(jnp.int32, late_ref.shape[1:], 0) == 0
    for ci in range(taps_ref.shape[0]):
        taps = taps_ref[pl.ds(ci, 1), :].astype(jnp.float32)
        low = jnp.broadcast_to(taps[:, :half], (half, half))
        high = jnp.broadcast_to(taps[:, half:], (half, half))
        low = pltpu.roll(low, 0, 1, stride=1, stride_axis=0)
        high = pltpu.roll(high, 0, 1, stride=1, stride_axis=0)
        d0 = jnp.where(upper, zero, high).astype(jnp.bfloat16)
        d1 = jnp.where(upper, high, low).astype(jnp.bfloat16)
        d2 = jnp.where(upper, low, zero).astype(jnp.bfloat16)
        none = jnp.zeros_like(d0)
        top = jnp.concatenate(
            [jnp.concatenate([d0, none], axis=1), jnp.concatenate([d1, d0], axis=1)], axis=0
        )
        bottom = jnp.concatenate(
            [jnp.concatenate([d2, d1], axis=1), jnp.concatenate([none, d2], axis=1)], axis=0
        )
        late = late_ref[ci]
        shifted_down = pltpu.roll(jnp.dot(late, top, preferred_element_type=jnp.float32), 1, 0)
        head = jnp.dot(previous_ref[pl.ds(ci, 1), :], top, preferred_element_type=jnp.float32)
        acc = jnp.where(first, jnp.broadcast_to(head, shifted_down.shape), shifted_down)
        acc = acc + jnp.dot(late, bottom, preferred_element_type=jnp.float32)
        out_ref[ci] = acc.astype(out_ref.dtype)


def whiten(fir_taps, previous, late):
    channels, nblocks, tap_count = late.shape
    group = 16 if channels % 16 == 0 else channels
    block = pl.BlockSpec((group, nblocks, tap_count), lambda g: (g, 0, 0))
    rows = pl.BlockSpec((group, tap_count), lambda g: (g, 0))
    return pl.pallas_call(
        fir_kernel,
        out_shape=jax.ShapeDtypeStruct(late.shape, jnp.bfloat16),
        grid=(channels // group,),
        in_specs=[rows, rows, block],
        out_specs=block,
        cost_estimate=pl.CostEstimate(
            flops=4 * channels * nblocks * tap_count * tap_count,
            bytes_accessed=2 * late.size * 2 + 2 * fir_taps.size * 2,
            transcendentals=0,
        ),
    )(fir_taps, previous, late)


def shards(strain, fir_taps):
    tap_count = fir_taps.shape[1]
    channels = strain.shape[0]
    previous = shifted(strain[:, -tap_count:], "tm", 1)
    late = strain.reshape(channels, -1, tap_count)
    whitened = whiten(fir_taps, previous, late).reshape(channels, -1)
    segments = whitened.reshape(channels * (whitened.shape[1] // SEG), SEG)
    parts = lax.axis_size("tm")
    table = make_table()
    bins = table.shape[2]
    table = jnp.asarray(
        table.reshape(SEG, 2, parts, bins // parts // 2, 2)
        .transpose(0, 2, 3, 4, 1)
        .reshape(SEG, 2 * bins)
    )
    spectra = jnp.einsum(
        "xn,nq->qx", segments, table, preferred_element_type=jnp.float32
    ).astype(jnp.bfloat16)
    pairs = bins // parts // 2
    spectra = spectra.reshape(parts, pairs, 4, spectra.shape[1])
    own = lax.all_to_all(spectra, "tm", split_axis=0, concat_axis=1, tiled=False)
    segs = own.shape[-1] // channels
    shard = own.reshape(pairs, 4 * parts, channels, segs).transpose(0, 2, 1, 3)
    shard = shard.reshape(pairs, channels, -1)
    every = lax.all_gather(shard, "chan", axis=0)
    return cross_spectra(lhs_rows(shard, parts), every)


def lhs_rows(shard, parts):
    pairs, channels, lanes = shard.shape
    split = shard.reshape(pairs, channels, parts, 2, 2, lanes // 4 // parts)
    parity = lax.broadcasted_iota(jnp.int32, split.shape, 3)
    zero = jnp.zeros_like(split)
    swapped = jnp.concatenate([split[:, :, :, :, 1:], -split[:, :, :, :, :1]], axis=4)
    rows = []
    for part in (split, swapped):
        for b in range(2):
            rows.append(jnp.where(parity == b, part, zero).reshape(pairs, channels, lanes))
    return jnp.stack(rows, axis=1).reshape(pairs, 4 * channels, lanes)


def cross_kernel(lhs_ref, every_ref, out_ref):
    sources, count, channels, lanes = every_ref.shape
    factor = 1.0 / (lanes // 4 * SEG)
    for t in range(count):
        rhs = every_ref[:, t].reshape(sources * channels, lanes)
        prod = lax.dot_general(
            lhs_ref[t], rhs, (((1,), (1,)), ((), ())), preferred_element_type=jnp.float32
        )
        prod = prod * factor
        for q in range(4):
            out_ref[q // 2, 2 * t + q % 2] = prod[q * channels:(q + 1) * channels]


def cross_spectra(lhs, every):
    sources, pairs, channels, lanes = every.shape
    step = 16 if pairs % 16 == 0 else pairs
    wide = sources * channels
    return pl.pallas_call(
        cross_kernel,
        out_shape=jax.ShapeDtypeStruct((2, 2 * pairs, channels, wide), jnp.float32),
        grid=(pairs // step,),
        in_specs=[
            pl.BlockSpec((step, 4 * channels, lanes), lambda g: (g, 0, 0)),
            pl.BlockSpec((sources, step, channels, lanes), lambda g: (0, g, 0, 0)),
        ],
        out_specs=pl.BlockSpec((2, 2 * step, channels, wide), lambda g: (0, g, 0, 0)),
        cost_estimate=pl.CostEstimate(
            flops=2 * pairs * 4 * channels * lanes * wide,
            bytes_accessed=lhs.size * 2 + every.size * 2 + 2 * 2 * pairs * channels * wide * 4,
            transcendentals=0,
        ),
    )(lhs, every)


def solution(mesh):
    placed = (P("chan", "tm"), P("chan", None))
    return jax.shard_map(
        shards, mesh=mesh, in_specs=placed, out_specs=P(None, "tm", "chan", None), check_vma=False
    )
```

```python
import functools
import math

import jax
import ml_dtypes
import numpy as np
import jax.numpy as jnp
from jax import lax
from jax.experimental import pallas as pl
from jax.experimental.pallas import tpu as pltpu
from jax.sharding import PartitionSpec as P

SEG = 512


def shifted(value, axis, by):
    size = lax.axis_size(axis)
    pairs = [(i, i + by) for i in range(size) if 0 <= i + by < size]
    return lax.ppermute(value, axis, pairs)


def make_table():
    sample_idx = np.arange(SEG, dtype=np.int32)
    bin_idx = np.arange(SEG // 2, dtype=np.int32)
    phases = sample_idx[:, None] * bin_idx[None, :] % SEG
    step = np.float32(2.0 * math.pi / SEG)
    angles = phases.astype(np.float32) * step
    window = np.float32(0.5) - np.float32(0.5) * np.cos(sample_idx.astype(np.float32) * step)
    cosine = window[:, None] * np.cos(angles)
    sine_part = -window[:, None] * np.sin(angles)
    return np.stack([cosine, sine_part], axis=1).astype(ml_dtypes.bfloat16)


def toeplitz(fir_taps):
    tap_count = fir_taps.shape[1]
    row_idx = jnp.arange(2 * tap_count, dtype=jnp.int32)[:, None]
    col_idx = jnp.arange(tap_count, dtype=jnp.int32)[None, :]
    lag_idx = col_idx + tap_count - row_idx
    valid = (lag_idx >= 0) & (lag_idx < tap_count)
    picked = jnp.take(fir_taps, jnp.clip(lag_idx, 0, tap_count - 1), axis=1)
    return jnp.where(valid[None, :, :], picked, jnp.zeros_like(picked))


def cross_block(own_bins, other_bins):
    swapped = jnp.stack([-other_bins[:, 1], other_bins[:, 0]], axis=1)
    real_part = jnp.einsum(
        "kpsi,kpsj->kij", own_bins, other_bins, preferred_element_type=jnp.float32
    )
    imag_part = jnp.einsum("kpsi,kpsj->kij", own_bins, swapped, preferred_element_type=jnp.float32)
    return jnp.stack([real_part, imag_part], axis=0)


def fir_kernel(taps_ref, previous_ref, late_ref, out_ref):
    half = taps_ref.shape[1] // 2
    row = lax.broadcasted_iota(jnp.int32, (half, half), 0)
    col = lax.broadcasted_iota(jnp.int32, (half, half), 1)
    upper = col >= row
    zero = jnp.zeros((half, half), jnp.float32)
    first = lax.broadcasted_iota(jnp.int32, late_ref.shape[1:], 0) == 0
    for ci in range(taps_ref.shape[0]):
        taps = taps_ref[pl.ds(ci, 1), :].astype(jnp.float32)
        low = jnp.broadcast_to(taps[:, :half], (half, half))
        high = jnp.broadcast_to(taps[:, half:], (half, half))
        low = pltpu.roll(low, 0, 1, stride=1, stride_axis=0)
        high = pltpu.roll(high, 0, 1, stride=1, stride_axis=0)
        d0 = jnp.where(upper, zero, high).astype(jnp.bfloat16)
        d1 = jnp.where(upper, high, low).astype(jnp.bfloat16)
        d2 = jnp.where(upper, low, zero).astype(jnp.bfloat16)
        none = jnp.zeros_like(d0)
        top = jnp.concatenate(
            [jnp.concatenate([d0, none], axis=1), jnp.concatenate([d1, d0], axis=1)], axis=0
        )
        bottom = jnp.concatenate(
            [jnp.concatenate([d2, d1], axis=1), jnp.concatenate([none, d2], axis=1)], axis=0
        )
        late = late_ref[ci]
        shifted_down = pltpu.roll(jnp.dot(late, top, preferred_element_type=jnp.float32), 1, 0)
        head = jnp.dot(previous_ref[pl.ds(ci, 1), :], top, preferred_element_type=jnp.float32)
        acc = jnp.where(first, jnp.broadcast_to(head, shifted_down.shape), shifted_down)
        acc = acc + jnp.dot(late, bottom, preferred_element_type=jnp.float32)
        out_ref[ci] = acc.astype(out_ref.dtype)


def whiten(fir_taps, previous, late):
    channels, nblocks, tap_count = late.shape
    group = 16 if channels % 16 == 0 else channels
    block = pl.BlockSpec((group, nblocks, tap_count), lambda g: (g, 0, 0))
    rows = pl.BlockSpec((group, tap_count), lambda g: (g, 0))
    return pl.pallas_call(
        fir_kernel,
        out_shape=jax.ShapeDtypeStruct(late.shape, jnp.bfloat16),
        grid=(channels // group,),
        in_specs=[rows, rows, block],
        out_specs=block,
        cost_estimate=pl.CostEstimate(
            flops=4 * channels * nblocks * tap_count * tap_count,
            bytes_accessed=2 * late.size * 2 + 2 * fir_taps.size * 2,
            transcendentals=0,
        ),
    )(fir_taps, previous, late)


def shards(strain, fir_taps):
    tap_count = fir_taps.shape[1]
    channels = strain.shape[0]
    previous = shifted(strain[:, -tap_count:], "tm", 1)
    late = strain.reshape(channels, -1, tap_count)
    whitened = whiten(fir_taps, previous, late).reshape(channels, -1)
    segments = whitened.reshape(channels * (whitened.shape[1] // SEG), SEG)
    parts = lax.axis_size("tm")
    table = make_table()
    bins = table.shape[2]
    table = jnp.asarray(
        table.reshape(SEG, 2, parts, bins // parts // 2, 2)
        .transpose(0, 2, 3, 4, 1)
        .reshape(SEG, 2 * bins)
    )
    spectra = jnp.einsum(
        "xn,nq->qx", segments, table, preferred_element_type=jnp.float32
    ).astype(jnp.bfloat16)
    pairs = bins // parts // 2
    spectra = spectra.reshape(parts, pairs, 4, spectra.shape[1])
    own = lax.all_to_all(spectra, "tm", split_axis=0, concat_axis=1, tiled=False)
    segs = own.shape[-1] // channels
    shard = own.reshape(pairs, 4 * parts, channels, segs).transpose(0, 2, 1, 3)
    shard = shard.reshape(pairs, channels, -1)
    every = lax.all_gather(shard, "chan", axis=0)
    return cross_spectra(shard, every, parts)


def cross_kernel(parts, own_ref, every_ref, out_ref):
    sources, count, channels, lanes = every_ref.shape
    segs = lanes // 4 // parts
    factor = 1.0 / (lanes // 4 * SEG)
    lane = lax.broadcasted_iota(jnp.int32, (channels, lanes), 1)
    parity = (lane // (2 * segs)) % 2
    second = (lane // segs) % 2 == 1
    for t in range(count):
        own = own_ref[t].astype(jnp.float32)
        later = pltpu.roll(own, lanes - segs, 1)
        earlier = pltpu.roll(own, segs, 1)
        swapped = jnp.where(second, -earlier, later)
        rows = []
        for part in (own, swapped):
            for b in range(2):
                rows.append(jnp.where(parity == b, part, 0.0))
        lhs = jnp.concatenate(rows, axis=0).astype(jnp.bfloat16)
        rhs = every_ref[:, t].reshape(sources * channels, lanes)
        prod = lax.dot_general(
            lhs, rhs, (((1,), (1,)), ((), ())), preferred_element_type=jnp.float32
        )
        prod = prod * factor
        for q in range(4):
            out_ref[q // 2, 2 * t + q % 2] = prod[q * channels:(q + 1) * channels]


def cross_spectra(own, every, parts):
    sources, pairs, channels, lanes = every.shape
    step = 16 if pairs % 16 == 0 else pairs
    wide = sources * channels
    return pl.pallas_call(
        functools.partial(cross_kernel, parts),
        out_shape=jax.ShapeDtypeStruct((2, 2 * pairs, channels, wide), jnp.float32),
        grid=(pairs // step,),
        in_specs=[
            pl.BlockSpec((step, channels, lanes), lambda g: (g, 0, 0)),
            pl.BlockSpec((sources, step, channels, lanes), lambda g: (0, g, 0, 0)),
        ],
        out_specs=pl.BlockSpec((2, 2 * step, channels, wide), lambda g: (0, g, 0, 0)),
        cost_estimate=pl.CostEstimate(
            flops=2 * pairs * 4 * channels * lanes * wide,
            bytes_accessed=own.size * 2 + every.size * 2 + 2 * 2 * pairs * channels * wide * 4,
            transcendentals=0,
        ),
    )(own, every)


def solution(mesh):
    placed = (P("chan", "tm"), P("chan", None))
    return jax.shard_map(
        shards, mesh=mesh, in_specs=placed, out_specs=P(None, "tm", "chan", None), check_vma=False
    )
```

```python
import functools
import math

import jax
import ml_dtypes
import numpy as np
import jax.numpy as jnp
from jax import lax
from jax.experimental import pallas as pl
from jax.experimental.pallas import tpu as pltpu
from jax.sharding import PartitionSpec as P

SEG = 512


def shifted(value, axis, by):
    size = lax.axis_size(axis)
    pairs = [(i, i + by) for i in range(size) if 0 <= i + by < size]
    return lax.ppermute(value, axis, pairs)


def make_table():
    sample_idx = np.arange(SEG, dtype=np.int32)
    bin_idx = np.arange(SEG // 2, dtype=np.int32)
    phases = sample_idx[:, None] * bin_idx[None, :] % SEG
    step = np.float32(2.0 * math.pi / SEG)
    angles = phases.astype(np.float32) * step
    window = np.float32(0.5) - np.float32(0.5) * np.cos(sample_idx.astype(np.float32) * step)
    cosine = window[:, None] * np.cos(angles)
    sine_part = -window[:, None] * np.sin(angles)
    return np.stack([cosine, sine_part], axis=1).astype(ml_dtypes.bfloat16)


def toeplitz(fir_taps):
    tap_count = fir_taps.shape[1]
    row_idx = jnp.arange(2 * tap_count, dtype=jnp.int32)[:, None]
    col_idx = jnp.arange(tap_count, dtype=jnp.int32)[None, :]
    lag_idx = col_idx + tap_count - row_idx
    valid = (lag_idx >= 0) & (lag_idx < tap_count)
    picked = jnp.take(fir_taps, jnp.clip(lag_idx, 0, tap_count - 1), axis=1)
    return jnp.where(valid[None, :, :], picked, jnp.zeros_like(picked))


def cross_block(own_bins, other_bins):
    swapped = jnp.stack([-other_bins[:, 1], other_bins[:, 0]], axis=1)
    real_part = jnp.einsum(
        "kpsi,kpsj->kij", own_bins, other_bins, preferred_element_type=jnp.float32
    )
    imag_part = jnp.einsum("kpsi,kpsj->kij", own_bins, swapped, preferred_element_type=jnp.float32)
    return jnp.stack([real_part, imag_part], axis=0)


def fir_kernel(taps_ref, previous_ref, late_ref, out_ref):
    half = taps_ref.shape[1] // 2
    row = lax.broadcasted_iota(jnp.int32, (half, half), 0)
    col = lax.broadcasted_iota(jnp.int32, (half, half), 1)
    upper = col >= row
    zero = jnp.zeros((half, half), jnp.float32)
    first = lax.broadcasted_iota(jnp.int32, late_ref.shape[1:], 0) == 0
    for ci in range(taps_ref.shape[0]):
        taps = taps_ref[pl.ds(ci, 1), :].astype(jnp.float32)
        low = jnp.broadcast_to(taps[:, :half], (half, half))
        high = jnp.broadcast_to(taps[:, half:], (half, half))
        low = pltpu.roll(low, 0, 1, stride=1, stride_axis=0)
        high = pltpu.roll(high, 0, 1, stride=1, stride_axis=0)
        d0 = jnp.where(upper, zero, high).astype(jnp.bfloat16)
        d1 = jnp.where(upper, high, low).astype(jnp.bfloat16)
        d2 = jnp.where(upper, low, zero).astype(jnp.bfloat16)
        none = jnp.zeros_like(d0)
        top = jnp.concatenate(
            [jnp.concatenate([d0, none], axis=1), jnp.concatenate([d1, d0], axis=1)], axis=0
        )
        bottom = jnp.concatenate(
            [jnp.concatenate([d2, d1], axis=1), jnp.concatenate([none, d2], axis=1)], axis=0
        )
        late = late_ref[ci]
        shifted_down = pltpu.roll(jnp.dot(late, top, preferred_element_type=jnp.float32), 1, 0)
        head = jnp.dot(previous_ref[pl.ds(ci, 1), :], top, preferred_element_type=jnp.float32)
        acc = jnp.where(first, jnp.broadcast_to(head, shifted_down.shape), shifted_down)
        acc = acc + jnp.dot(late, bottom, preferred_element_type=jnp.float32)
        out_ref[ci] = acc.astype(out_ref.dtype)


def whiten(fir_taps, previous, late):
    channels, nblocks, tap_count = late.shape
    group = channels
    block = pl.BlockSpec((group, nblocks, tap_count), lambda g: (g, 0, 0))
    rows = pl.BlockSpec((group, tap_count), lambda g: (g, 0))
    return pl.pallas_call(
        fir_kernel,
        out_shape=jax.ShapeDtypeStruct(late.shape, jnp.bfloat16),
        grid=(channels // group,),
        in_specs=[rows, rows, block],
        out_specs=block,
        cost_estimate=pl.CostEstimate(
            flops=4 * channels * nblocks * tap_count * tap_count,
            bytes_accessed=2 * late.size * 2 + 2 * fir_taps.size * 2,
            transcendentals=0,
        ),
    )(fir_taps, previous, late)


def shards(strain, fir_taps):
    tap_count = fir_taps.shape[1]
    channels = strain.shape[0]
    previous = shifted(strain[:, -tap_count:], "tm", 1)
    late = strain.reshape(channels, -1, tap_count)
    whitened = whiten(fir_taps, previous, late).reshape(channels, -1)
    segments = whitened.reshape(channels * (whitened.shape[1] // SEG), SEG)
    parts = lax.axis_size("tm")
    table = make_table()
    bins = table.shape[2]
    table = jnp.asarray(
        table.reshape(SEG, 2, parts, bins // parts // 2, 2)
        .transpose(0, 2, 3, 4, 1)
        .reshape(SEG, 2 * bins)
    )
    spectra = jnp.einsum(
        "xn,nq->qx", segments, table, preferred_element_type=jnp.float32
    ).astype(jnp.bfloat16)
    pairs = bins // parts // 2
    spectra = spectra.reshape(parts, pairs, 4, spectra.shape[1])
    own = lax.all_to_all(spectra, "tm", split_axis=0, concat_axis=1, tiled=False)
    segs = own.shape[-1] // channels
    shard = own.reshape(pairs, 4 * parts, channels, segs).transpose(0, 2, 1, 3)
    shard = shard.reshape(pairs, channels, -1)
    every = lax.all_gather(shard, "chan", axis=0)
    return cross_spectra(shard, every, parts)


def cross_kernel(parts, own_ref, every_ref, out_ref):
    sources, count, channels, lanes = every_ref.shape
    segs = lanes // 4 // parts
    factor = 1.0 / (lanes // 4 * SEG)
    lane = lax.broadcasted_iota(jnp.int32, (channels, lanes), 1)
    parity = (lane // (2 * segs)) % 2
    second = (lane // segs) % 2 == 1
    for t in range(count):
        own = own_ref[t].astype(jnp.float32)
        later = pltpu.roll(own, lanes - segs, 1)
        earlier = pltpu.roll(own, segs, 1)
        swapped = jnp.where(second, -earlier, later)
        rows = []
        for part in (own, swapped):
            for b in range(2):
                rows.append(jnp.where(parity == b, part, 0.0))
        lhs = jnp.concatenate(rows, axis=0).astype(jnp.bfloat16)
        rhs = every_ref[:, t].reshape(sources * channels, lanes)
        prod = lax.dot_general(
            lhs, rhs, (((1,), (1,)), ((), ())), preferred_element_type=jnp.float32
        )
        prod = prod * factor
        for q in range(4):
            out_ref[q // 2, 2 * t + q % 2] = prod[q * channels:(q + 1) * channels]


def cross_spectra(own, every, parts):
    sources, pairs, channels, lanes = every.shape
    step = 16 if pairs % 16 == 0 else pairs
    wide = sources * channels
    return pl.pallas_call(
        functools.partial(cross_kernel, parts),
        out_shape=jax.ShapeDtypeStruct((2, 2 * pairs, channels, wide), jnp.float32),
        grid=(pairs // step,),
        in_specs=[
            pl.BlockSpec((step, channels, lanes), lambda g: (g, 0, 0)),
            pl.BlockSpec((sources, step, channels, lanes), lambda g: (0, g, 0, 0)),
        ],
        out_specs=pl.BlockSpec((2, 2 * step, channels, wide), lambda g: (0, g, 0, 0)),
        cost_estimate=pl.CostEstimate(
            flops=2 * pairs * 4 * channels * lanes * wide,
            bytes_accessed=own.size * 2 + every.size * 2 + 2 * 2 * pairs * channels * wide * 4,
            transcendentals=0,
        ),
    )(own, every)


def solution(mesh):
    placed = (P("chan", "tm"), P("chan", None))
    return jax.shard_map(
        shards, mesh=mesh, in_specs=placed, out_specs=P(None, "tm", "chan", None), check_vma=False
    )
```

```python
import functools
import math

import jax
import ml_dtypes
import numpy as np
import jax.numpy as jnp
from jax import lax
from jax.experimental import pallas as pl
from jax.experimental.pallas import tpu as pltpu
from jax.sharding import PartitionSpec as P

SEG = 512


def shifted(value, axis, by):
    size = lax.axis_size(axis)
    pairs = [(i, i + by) for i in range(size) if 0 <= i + by < size]
    return lax.ppermute(value, axis, pairs)


def make_table():
    sample_idx = np.arange(SEG, dtype=np.int32)
    bin_idx = np.arange(SEG // 2, dtype=np.int32)
    phases = sample_idx[:, None] * bin_idx[None, :] % SEG
    step = np.float32(2.0 * math.pi / SEG)
    angles = phases.astype(np.float32) * step
    window = np.float32(0.5) - np.float32(0.5) * np.cos(sample_idx.astype(np.float32) * step)
    cosine = window[:, None] * np.cos(angles)
    sine_part = -window[:, None] * np.sin(angles)
    return np.stack([cosine, sine_part], axis=1).astype(ml_dtypes.bfloat16)


def toeplitz(fir_taps):
    tap_count = fir_taps.shape[1]
    row_idx = jnp.arange(2 * tap_count, dtype=jnp.int32)[:, None]
    col_idx = jnp.arange(tap_count, dtype=jnp.int32)[None, :]
    lag_idx = col_idx + tap_count - row_idx
    valid = (lag_idx >= 0) & (lag_idx < tap_count)
    picked = jnp.take(fir_taps, jnp.clip(lag_idx, 0, tap_count - 1), axis=1)
    return jnp.where(valid[None, :, :], picked, jnp.zeros_like(picked))


def cross_block(own_bins, other_bins):
    swapped = jnp.stack([-other_bins[:, 1], other_bins[:, 0]], axis=1)
    real_part = jnp.einsum(
        "kpsi,kpsj->kij", own_bins, other_bins, preferred_element_type=jnp.float32
    )
    imag_part = jnp.einsum("kpsi,kpsj->kij", own_bins, swapped, preferred_element_type=jnp.float32)
    return jnp.stack([real_part, imag_part], axis=0)


def fir_kernel(taps_ref, previous_ref, late_ref, out_ref):
    half = taps_ref.shape[1] // 2
    row = lax.broadcasted_iota(jnp.int32, (half, half), 0)
    col = lax.broadcasted_iota(jnp.int32, (half, half), 1)
    upper = col >= row
    zero = jnp.zeros((half, half), jnp.float32)
    first = lax.broadcasted_iota(jnp.int32, late_ref.shape[1:], 0) == 0
    for ci in range(taps_ref.shape[0]):
        taps = taps_ref[pl.ds(ci, 1), :].astype(jnp.float32)
        low = jnp.broadcast_to(taps[:, :half], (half, half))
        high = jnp.broadcast_to(taps[:, half:], (half, half))
        low = pltpu.roll(low, 0, 1, stride=1, stride_axis=0)
        high = pltpu.roll(high, 0, 1, stride=1, stride_axis=0)
        d0 = jnp.where(upper, zero, high).astype(jnp.bfloat16)
        d1 = jnp.where(upper, high, low).astype(jnp.bfloat16)
        d2 = jnp.where(upper, low, zero).astype(jnp.bfloat16)
        none = jnp.zeros_like(d0)
        top = jnp.concatenate(
            [jnp.concatenate([d0, none], axis=1), jnp.concatenate([d1, d0], axis=1)], axis=0
        )
        bottom = jnp.concatenate(
            [jnp.concatenate([d2, d1], axis=1), jnp.concatenate([none, d2], axis=1)], axis=0
        )
        late = late_ref[ci]
        shifted_down = pltpu.roll(jnp.dot(late, top, preferred_element_type=jnp.float32), 1, 0)
        head = jnp.dot(previous_ref[pl.ds(ci, 1), :], top, preferred_element_type=jnp.float32)
        acc = jnp.where(first, jnp.broadcast_to(head, shifted_down.shape), shifted_down)
        acc = acc + jnp.dot(late, bottom, preferred_element_type=jnp.float32)
        out_ref[ci] = acc.astype(out_ref.dtype)


def whiten(fir_taps, previous, late):
    channels, nblocks, tap_count = late.shape
    group = 16 if channels % 16 == 0 else channels
    block = pl.BlockSpec((group, nblocks, tap_count), lambda g: (g, 0, 0))
    rows = pl.BlockSpec((group, tap_count), lambda g: (g, 0))
    return pl.pallas_call(
        fir_kernel,
        out_shape=jax.ShapeDtypeStruct(late.shape, jnp.bfloat16),
        grid=(channels // group,),
        in_specs=[rows, rows, block],
        out_specs=block,
        cost_estimate=pl.CostEstimate(
            flops=4 * channels * nblocks * tap_count * tap_count,
            bytes_accessed=2 * late.size * 2 + 2 * fir_taps.size * 2,
            transcendentals=0,
        ),
    )(fir_taps, previous, late)


def shards(strain, fir_taps):
    tap_count = fir_taps.shape[1]
    channels = strain.shape[0]
    previous = shifted(strain[:, -tap_count:], "tm", 1)
    late = strain.reshape(channels, -1, tap_count)
    whitened = whiten(fir_taps, previous, late).reshape(channels, -1)
    segments = whitened.reshape(channels * (whitened.shape[1] // SEG), SEG)
    parts = lax.axis_size("tm")
    table = make_table()
    bins = table.shape[2]
    table = jnp.asarray(
        table.reshape(SEG, 2, parts, bins // parts // 2, 2)
        .transpose(0, 2, 3, 4, 1)
        .reshape(SEG, 2 * bins)
    )
    spectra = jnp.einsum(
        "xn,nq->qx", segments, table, preferred_element_type=jnp.float32
    ).astype(jnp.bfloat16)
    pairs = bins // parts // 2
    spectra = spectra.reshape(parts, pairs, 4, spectra.shape[1])
    own = lax.all_to_all(spectra, "tm", split_axis=0, concat_axis=1, tiled=False)
    segs = own.shape[-1] // channels
    shard = own.reshape(pairs, 4 * parts, channels, segs).transpose(0, 2, 1, 3)
    shard = shard.reshape(pairs, channels, -1)
    every = lax.all_gather(shard, "chan", axis=0)
    return cross_spectra(shard, every, parts)


def cross_kernel(parts, own_ref, every_ref, out_ref):
    sources, count, channels, lanes = every_ref.shape
    segs = lanes // 4 // parts
    factor = 1.0 / (lanes // 4 * SEG)
    lane = lax.broadcasted_iota(jnp.int32, (channels, lanes), 1)
    parity = (lane // (2 * segs)) % 2
    second = (lane // segs) % 2 == 1
    for t in range(count):
        own = own_ref[t].astype(jnp.float32)
        later = pltpu.roll(own, lanes - segs, 1)
        earlier = pltpu.roll(own, segs, 1)
        swapped = jnp.where(second, -earlier, later)
        rows = []
        for part in (own, swapped):
            for b in range(2):
                rows.append(jnp.where(parity == b, part, 0.0))
        lhs = jnp.concatenate(rows, axis=0).astype(jnp.bfloat16)
        rhs = every_ref[:, t].reshape(sources * channels, lanes)
        prod = lax.dot_general(
            lhs, rhs, (((1,), (1,)), ((), ())), preferred_element_type=jnp.float32
        )
        prod = prod * factor
        for q in range(4):
            out_ref[q // 2, 2 * t + q % 2] = prod[q * channels:(q + 1) * channels]


def cross_spectra(own, every, parts):
    sources, pairs, channels, lanes = every.shape
    step = pairs
    wide = sources * channels
    return pl.pallas_call(
        functools.partial(cross_kernel, parts),
        out_shape=jax.ShapeDtypeStruct((2, 2 * pairs, channels, wide), jnp.float32),
        grid=(pairs // step,),
        in_specs=[
            pl.BlockSpec((step, channels, lanes), lambda g: (g, 0, 0)),
            pl.BlockSpec((sources, step, channels, lanes), lambda g: (0, g, 0, 0)),
        ],
        out_specs=pl.BlockSpec((2, 2 * step, channels, wide), lambda g: (0, g, 0, 0)),
        cost_estimate=pl.CostEstimate(
            flops=2 * pairs * 4 * channels * lanes * wide,
            bytes_accessed=own.size * 2 + every.size * 2 + 2 * 2 * pairs * channels * wide * 4,
            transcendentals=0,
        ),
    )(own, every)


def solution(mesh):
    placed = (P("chan", "tm"), P("chan", None))
    return jax.shard_map(
        shards, mesh=mesh, in_specs=placed, out_specs=P(None, "tm", "chan", None), check_vma=False
    )
```

```python
import functools
import math

import jax
import ml_dtypes
import numpy as np
import jax.numpy as jnp
from jax import lax
from jax.experimental import pallas as pl
from jax.experimental.pallas import tpu as pltpu
from jax.sharding import PartitionSpec as P

SEG = 512


def shifted(value, axis, by):
    size = lax.axis_size(axis)
    pairs = [(i, i + by) for i in range(size) if 0 <= i + by < size]
    return lax.ppermute(value, axis, pairs)


def make_table():
    sample_idx = np.arange(SEG, dtype=np.int32)
    bin_idx = np.arange(SEG // 2, dtype=np.int32)
    phases = sample_idx[:, None] * bin_idx[None, :] % SEG
    step = np.float32(2.0 * math.pi / SEG)
    angles = phases.astype(np.float32) * step
    window = np.float32(0.5) - np.float32(0.5) * np.cos(sample_idx.astype(np.float32) * step)
    cosine = window[:, None] * np.cos(angles)
    sine_part = -window[:, None] * np.sin(angles)
    return np.stack([cosine, sine_part], axis=1).astype(ml_dtypes.bfloat16)


def toeplitz(fir_taps):
    tap_count = fir_taps.shape[1]
    row_idx = jnp.arange(2 * tap_count, dtype=jnp.int32)[:, None]
    col_idx = jnp.arange(tap_count, dtype=jnp.int32)[None, :]
    lag_idx = col_idx + tap_count - row_idx
    valid = (lag_idx >= 0) & (lag_idx < tap_count)
    picked = jnp.take(fir_taps, jnp.clip(lag_idx, 0, tap_count - 1), axis=1)
    return jnp.where(valid[None, :, :], picked, jnp.zeros_like(picked))


def cross_block(own_bins, other_bins):
    swapped = jnp.stack([-other_bins[:, 1], other_bins[:, 0]], axis=1)
    real_part = jnp.einsum(
        "kpsi,kpsj->kij", own_bins, other_bins, preferred_element_type=jnp.float32
    )
    imag_part = jnp.einsum("kpsi,kpsj->kij", own_bins, swapped, preferred_element_type=jnp.float32)
    return jnp.stack([real_part, imag_part], axis=0)


def fir_kernel(taps_ref, previous_ref, seg_ref, out_ref):
    half = taps_ref.shape[1] // 2
    row = lax.broadcasted_iota(jnp.int32, (half, half), 0)
    col = lax.broadcasted_iota(jnp.int32, (half, half), 1)
    upper = col >= row
    zero = jnp.zeros((half, half), jnp.float32)
    for ci in range(taps_ref.shape[0]):
        taps = taps_ref[pl.ds(ci, 1), :].astype(jnp.float32)
        low = jnp.broadcast_to(taps[:, :half], (half, half))
        high = jnp.broadcast_to(taps[:, half:], (half, half))
        low = pltpu.roll(low, 0, 1, stride=1, stride_axis=0)
        high = pltpu.roll(high, 0, 1, stride=1, stride_axis=0)
        d0 = jnp.where(upper, zero, high).astype(jnp.bfloat16)
        d1 = jnp.where(upper, high, low).astype(jnp.bfloat16)
        d2 = jnp.where(upper, low, zero).astype(jnp.bfloat16)
        none = jnp.zeros_like(d0)
        top = jnp.concatenate(
            [jnp.concatenate([d0, none], axis=1), jnp.concatenate([d1, d0], axis=1)], axis=0
        )
        bottom = jnp.concatenate(
            [jnp.concatenate([d2, d1], axis=1), jnp.concatenate([none, d2], axis=1)], axis=0
        )
        pair = seg_ref[ci].astype(jnp.float32)
        half_seg = pair.shape[1] // 2
        stacked = jnp.concatenate([pair[:, :half_seg], pair[:, half_seg:]], axis=0)
        stacked = stacked.astype(jnp.bfloat16)
        count = pair.shape[0]
        upper_part = jnp.dot(stacked, top, preferred_element_type=jnp.float32)
        lower_part = jnp.dot(stacked, bottom, preferred_element_type=jnp.float32)
        head = jnp.dot(previous_ref[pl.ds(ci, 1), :], top, preferred_element_type=jnp.float32)
        carried = pltpu.roll(upper_part[count:], 1, 0)
        first = lax.broadcasted_iota(jnp.int32, carried.shape, 0) == 0
        even = jnp.where(first, jnp.broadcast_to(head, carried.shape), carried) + lower_part[:count]
        odd = upper_part[:count] + lower_part[count:]
        out_ref[pl.ds(ci * count, count), :] = jnp.concatenate([even, odd], axis=1).astype(
            out_ref.dtype
        )


def whiten(fir_taps, previous, segs):
    channels, count, width = segs.shape
    tap_count = fir_taps.shape[1]
    group = channels
    rows = pl.BlockSpec((group, tap_count), lambda g: (g, 0))
    return pl.pallas_call(
        fir_kernel,
        out_shape=jax.ShapeDtypeStruct((channels * count, width), jnp.bfloat16),
        grid=(channels // group,),
        in_specs=[rows, rows, pl.BlockSpec((group, count, width), lambda g: (g, 0, 0))],
        out_specs=pl.BlockSpec((group * count, width), lambda g: (g, 0)),
        cost_estimate=pl.CostEstimate(
            flops=2 * channels * count * width * tap_count * 2,
            bytes_accessed=2 * segs.size * 2 + 2 * fir_taps.size * 2,
            transcendentals=0,
        ),
    )(fir_taps, previous, segs)


def shards(strain, fir_taps):
    tap_count = fir_taps.shape[1]
    channels = strain.shape[0]
    previous = shifted(strain[:, -tap_count:], "tm", 1)
    segments = whiten(fir_taps, previous, strain.reshape(channels, -1, SEG))
    parts = lax.axis_size("tm")
    table = make_table()
    bins = table.shape[2]
    table = jnp.asarray(
        table.reshape(SEG, 2, parts, bins // parts // 2, 2)
        .transpose(0, 2, 3, 4, 1)
        .reshape(SEG, 2 * bins)
    )
    spectra = jnp.einsum(
        "xn,nq->qx", segments, table, preferred_element_type=jnp.float32
    ).astype(jnp.bfloat16)
    pairs = bins // parts // 2
    spectra = spectra.reshape(parts, pairs, 4, spectra.shape[1])
    own = lax.all_to_all(spectra, "tm", split_axis=0, concat_axis=1, tiled=False)
    segs = own.shape[-1] // channels
    shard = own.reshape(pairs, 4 * parts, channels, segs).transpose(0, 2, 1, 3)
    shard = shard.reshape(pairs, channels, -1)
    every = lax.all_gather(shard, "chan", axis=0)
    return cross_spectra(shard, every, parts)


def cross_kernel(parts, own_ref, every_ref, out_ref):
    sources, count, channels, lanes = every_ref.shape
    segs = lanes // 4 // parts
    factor = 1.0 / (lanes // 4 * SEG)
    lane = lax.broadcasted_iota(jnp.int32, (channels, lanes), 1)
    parity = (lane // (2 * segs)) % 2
    second = (lane // segs) % 2 == 1
    for t in range(count):
        own = own_ref[t].astype(jnp.float32)
        later = pltpu.roll(own, lanes - segs, 1)
        earlier = pltpu.roll(own, segs, 1)
        swapped = jnp.where(second, -earlier, later)
        rows = []
        for part in (own, swapped):
            for b in range(2):
                rows.append(jnp.where(parity == b, part, 0.0))
        lhs = jnp.concatenate(rows, axis=0).astype(jnp.bfloat16)
        rhs = every_ref[:, t].reshape(sources * channels, lanes)
        prod = lax.dot_general(
            lhs, rhs, (((1,), (1,)), ((), ())), preferred_element_type=jnp.float32
        )
        prod = prod * factor
        for q in range(4):
            out_ref[q // 2, 2 * t + q % 2] = prod[q * channels:(q + 1) * channels]


def cross_spectra(own, every, parts):
    sources, pairs, channels, lanes = every.shape
    step = 16 if pairs % 16 == 0 else pairs
    wide = sources * channels
    return pl.pallas_call(
        functools.partial(cross_kernel, parts),
        out_shape=jax.ShapeDtypeStruct((2, 2 * pairs, channels, wide), jnp.float32),
        grid=(pairs // step,),
        in_specs=[
            pl.BlockSpec((step, channels, lanes), lambda g: (g, 0, 0)),
            pl.BlockSpec((sources, step, channels, lanes), lambda g: (0, g, 0, 0)),
        ],
        out_specs=pl.BlockSpec((2, 2 * step, channels, wide), lambda g: (0, g, 0, 0)),
        cost_estimate=pl.CostEstimate(
            flops=2 * pairs * 4 * channels * lanes * wide,
            bytes_accessed=own.size * 2 + every.size * 2 + 2 * 2 * pairs * channels * wide * 4,
            transcendentals=0,
        ),
    )(own, every)


def solution(mesh):
    placed = (P("chan", "tm"), P("chan", None))
    return jax.shard_map(
        shards, mesh=mesh, in_specs=placed, out_specs=P(None, "tm", "chan", None), check_vma=False
    )
```

```python
import functools
import math

import jax
import ml_dtypes
import numpy as np
import jax.numpy as jnp
from jax import lax
from jax.experimental import pallas as pl
from jax.experimental.pallas import tpu as pltpu
from jax.sharding import PartitionSpec as P

SEG = 512


def shifted(value, axis, by):
    size = lax.axis_size(axis)
    pairs = [(i, i + by) for i in range(size) if 0 <= i + by < size]
    return lax.ppermute(value, axis, pairs)


def make_table():
    sample_idx = np.arange(SEG, dtype=np.int32)
    bin_idx = np.arange(SEG // 2, dtype=np.int32)
    phases = sample_idx[:, None] * bin_idx[None, :] % SEG
    step = np.float32(2.0 * math.pi / SEG)
    angles = phases.astype(np.float32) * step
    window = np.float32(0.5) - np.float32(0.5) * np.cos(sample_idx.astype(np.float32) * step)
    cosine = window[:, None] * np.cos(angles)
    sine_part = -window[:, None] * np.sin(angles)
    return np.stack([cosine, sine_part], axis=1).astype(ml_dtypes.bfloat16)


def toeplitz(fir_taps):
    tap_count = fir_taps.shape[1]
    row_idx = jnp.arange(2 * tap_count, dtype=jnp.int32)[:, None]
    col_idx = jnp.arange(tap_count, dtype=jnp.int32)[None, :]
    lag_idx = col_idx + tap_count - row_idx
    valid = (lag_idx >= 0) & (lag_idx < tap_count)
    picked = jnp.take(fir_taps, jnp.clip(lag_idx, 0, tap_count - 1), axis=1)
    return jnp.where(valid[None, :, :], picked, jnp.zeros_like(picked))


def cross_block(own_bins, other_bins):
    swapped = jnp.stack([-other_bins[:, 1], other_bins[:, 0]], axis=1)
    real_part = jnp.einsum(
        "kpsi,kpsj->kij", own_bins, other_bins, preferred_element_type=jnp.float32
    )
    imag_part = jnp.einsum("kpsi,kpsj->kij", own_bins, swapped, preferred_element_type=jnp.float32)
    return jnp.stack([real_part, imag_part], axis=0)


def fir_kernel(taps_ref, previous_ref, seg_ref, table_ref, out_ref, whitened_ref):
    half = taps_ref.shape[1] // 2
    row = lax.broadcasted_iota(jnp.int32, (half, half), 0)
    col = lax.broadcasted_iota(jnp.int32, (half, half), 1)
    upper = col >= row
    zero = jnp.zeros((half, half), jnp.float32)
    for ci in range(taps_ref.shape[0]):
        taps = taps_ref[pl.ds(ci, 1), :].astype(jnp.float32)
        low = jnp.broadcast_to(taps[:, :half], (half, half))
        high = jnp.broadcast_to(taps[:, half:], (half, half))
        low = pltpu.roll(low, 0, 1, stride=1, stride_axis=0)
        high = pltpu.roll(high, 0, 1, stride=1, stride_axis=0)
        d0 = jnp.where(upper, zero, high).astype(jnp.bfloat16)
        d1 = jnp.where(upper, high, low).astype(jnp.bfloat16)
        d2 = jnp.where(upper, low, zero).astype(jnp.bfloat16)
        none = jnp.zeros_like(d0)
        top = jnp.concatenate(
            [jnp.concatenate([d0, none], axis=1), jnp.concatenate([d1, d0], axis=1)], axis=0
        )
        bottom = jnp.concatenate(
            [jnp.concatenate([d2, d1], axis=1), jnp.concatenate([none, d2], axis=1)], axis=0
        )
        pair = seg_ref[ci].astype(jnp.float32)
        half_seg = pair.shape[1] // 2
        stacked = jnp.concatenate([pair[:, :half_seg], pair[:, half_seg:]], axis=0)
        stacked = stacked.astype(jnp.bfloat16)
        count = pair.shape[0]
        upper_part = jnp.dot(stacked, top, preferred_element_type=jnp.float32)
        lower_part = jnp.dot(stacked, bottom, preferred_element_type=jnp.float32)
        head = jnp.dot(previous_ref[pl.ds(ci, 1), :], top, preferred_element_type=jnp.float32)
        carried = pltpu.roll(upper_part[count:], 1, 0)
        first = lax.broadcasted_iota(jnp.int32, carried.shape, 0) == 0
        even = jnp.where(first, jnp.broadcast_to(head, carried.shape), carried) + lower_part[:count]
        odd = upper_part[:count] + lower_part[count:]
        whitened_ref[pl.ds(ci * count, count), :] = jnp.concatenate([even, odd], axis=1).astype(
            whitened_ref.dtype
        )
    out_ref[...] = lax.dot_general(
        table_ref[...], whitened_ref[...], (((1,), (1,)), ((), ())), preferred_element_type=jnp.float32
    ).astype(out_ref.dtype)


def whiten(fir_taps, previous, segs, table):
    channels, count, width = segs.shape
    tap_count = fir_taps.shape[1]
    rows = pl.BlockSpec((channels, tap_count), lambda g: (0, 0))
    return pl.pallas_call(
        fir_kernel,
        out_shape=jax.ShapeDtypeStruct((table.shape[0], channels * count), jnp.bfloat16),
        grid=(1,),
        in_specs=[
            rows,
            rows,
            pl.BlockSpec((channels, count, width), lambda g: (0, 0, 0)),
            pl.BlockSpec(table.shape, lambda g: (0, 0)),
        ],
        out_specs=pl.BlockSpec((table.shape[0], channels * count), lambda g: (0, 0)),
        scratch_shapes=[pltpu.VMEM((channels * count, width), jnp.bfloat16)],
        cost_estimate=pl.CostEstimate(
            flops=2 * channels * count * width * (2 * tap_count + table.shape[0]),
            bytes_accessed=segs.size * 2 + 2 * fir_taps.size * 2 + table.size * 2 + segs.size * 2,
            transcendentals=0,
        ),
    )(fir_taps, previous, segs, table)


def shards(strain, fir_taps):
    tap_count = fir_taps.shape[1]
    channels = strain.shape[0]
    previous = shifted(strain[:, -tap_count:], "tm", 1)
    parts = lax.axis_size("tm")
    table = make_table()
    bins = table.shape[2]
    table = jnp.asarray(
        table.reshape(SEG, 2, parts, bins // parts // 2, 2)
        .transpose(0, 2, 3, 4, 1)
        .reshape(SEG, 2 * bins)
        .T
    )
    spectra = whiten(fir_taps, previous, strain.reshape(channels, -1, SEG), table)
    pairs = bins // parts // 2
    spectra = spectra.reshape(parts, pairs, 4, spectra.shape[1])
    own = lax.all_to_all(spectra, "tm", split_axis=0, concat_axis=1, tiled=False)
    segs = own.shape[-1] // channels
    shard = own.reshape(pairs, 4 * parts, channels, segs).transpose(0, 2, 1, 3)
    shard = shard.reshape(pairs, channels, -1)
    every = lax.all_gather(shard, "chan", axis=0)
    return cross_spectra(shard, every, parts)


def cross_kernel(parts, own_ref, every_ref, out_ref):
    sources, count, channels, lanes = every_ref.shape
    segs = lanes // 4 // parts
    factor = 1.0 / (lanes // 4 * SEG)
    lane = lax.broadcasted_iota(jnp.int32, (channels, lanes), 1)
    parity = (lane // (2 * segs)) % 2
    second = (lane // segs) % 2 == 1
    for t in range(count):
        own = own_ref[t].astype(jnp.float32)
        later = pltpu.roll(own, lanes - segs, 1)
        earlier = pltpu.roll(own, segs, 1)
        swapped = jnp.where(second, -earlier, later)
        rows = []
        for part in (own, swapped):
            for b in range(2):
                rows.append(jnp.where(parity == b, part, 0.0))
        lhs = jnp.concatenate(rows, axis=0).astype(jnp.bfloat16)
        rhs = every_ref[:, t].reshape(sources * channels, lanes)
        prod = lax.dot_general(
            lhs, rhs, (((1,), (1,)), ((), ())), preferred_element_type=jnp.float32
        )
        prod = prod * factor
        for q in range(4):
            out_ref[q // 2, 2 * t + q % 2] = prod[q * channels:(q + 1) * channels]


def cross_spectra(own, every, parts):
    sources, pairs, channels, lanes = every.shape
    step = 16 if pairs % 16 == 0 else pairs
    wide = sources * channels
    return pl.pallas_call(
        functools.partial(cross_kernel, parts),
        out_shape=jax.ShapeDtypeStruct((2, 2 * pairs, channels, wide), jnp.float32),
        grid=(pairs // step,),
        in_specs=[
            pl.BlockSpec((step, channels, lanes), lambda g: (g, 0, 0)),
            pl.BlockSpec((sources, step, channels, lanes), lambda g: (0, g, 0, 0)),
        ],
        out_specs=pl.BlockSpec((2, 2 * step, channels, wide), lambda g: (0, g, 0, 0)),
        cost_estimate=pl.CostEstimate(
            flops=2 * pairs * 4 * channels * lanes * wide,
            bytes_accessed=own.size * 2 + every.size * 2 + 2 * 2 * pairs * channels * wide * 4,
            transcendentals=0,
        ),
    )(own, every)


def solution(mesh):
    placed = (P("chan", "tm"), P("chan", None))
    return jax.shard_map(
        shards, mesh=mesh, in_specs=placed, out_specs=P(None, "tm", "chan", None), check_vma=False
    )
```

```python
import functools
import math

import jax
import ml_dtypes
import numpy as np
import jax.numpy as jnp
from jax import lax
from jax.experimental import pallas as pl
from jax.experimental.pallas import tpu as pltpu
from jax.sharding import PartitionSpec as P

SEG = 512


def shifted(value, axis, by):
    size = lax.axis_size(axis)
    pairs = [(i, i + by) for i in range(size) if 0 <= i + by < size]
    return lax.ppermute(value, axis, pairs)


def make_table():
    sample_idx = np.arange(SEG, dtype=np.int32)
    bin_idx = np.arange(SEG // 2, dtype=np.int32)
    phases = sample_idx[:, None] * bin_idx[None, :] % SEG
    step = np.float32(2.0 * math.pi / SEG)
    angles = phases.astype(np.float32) * step
    window = np.float32(0.5) - np.float32(0.5) * np.cos(sample_idx.astype(np.float32) * step)
    cosine = window[:, None] * np.cos(angles)
    sine_part = -window[:, None] * np.sin(angles)
    return np.stack([cosine, sine_part], axis=1).astype(ml_dtypes.bfloat16)


def toeplitz(fir_taps):
    tap_count = fir_taps.shape[1]
    row_idx = jnp.arange(2 * tap_count, dtype=jnp.int32)[:, None]
    col_idx = jnp.arange(tap_count, dtype=jnp.int32)[None, :]
    lag_idx = col_idx + tap_count - row_idx
    valid = (lag_idx >= 0) & (lag_idx < tap_count)
    picked = jnp.take(fir_taps, jnp.clip(lag_idx, 0, tap_count - 1), axis=1)
    return jnp.where(valid[None, :, :], picked, jnp.zeros_like(picked))


def cross_block(own_bins, other_bins):
    swapped = jnp.stack([-other_bins[:, 1], other_bins[:, 0]], axis=1)
    real_part = jnp.einsum(
        "kpsi,kpsj->kij", own_bins, other_bins, preferred_element_type=jnp.float32
    )
    imag_part = jnp.einsum("kpsi,kpsj->kij", own_bins, swapped, preferred_element_type=jnp.float32)
    return jnp.stack([real_part, imag_part], axis=0)


def fir_kernel(taps_ref, previous_ref, seg_ref, out_ref):
    half = taps_ref.shape[1] // 2
    row = lax.broadcasted_iota(jnp.int32, (half, half), 0)
    col = lax.broadcasted_iota(jnp.int32, (half, half), 1)
    upper = col >= row
    zero = jnp.zeros((half, half), jnp.float32)
    for ci in range(taps_ref.shape[0]):
        taps = taps_ref[pl.ds(ci, 1), :].astype(jnp.float32)
        low = jnp.broadcast_to(taps[:, :half], (half, half))
        high = jnp.broadcast_to(taps[:, half:], (half, half))
        low = pltpu.roll(low, 0, 1, stride=1, stride_axis=0)
        high = pltpu.roll(high, 0, 1, stride=1, stride_axis=0)
        d0 = jnp.where(upper, zero, high).astype(jnp.bfloat16)
        d1 = jnp.where(upper, high, low).astype(jnp.bfloat16)
        d2 = jnp.where(upper, low, zero).astype(jnp.bfloat16)
        none = jnp.zeros_like(d0)
        top = jnp.concatenate(
            [jnp.concatenate([d0, none], axis=1), jnp.concatenate([d1, d0], axis=1)], axis=0
        )
        bottom = jnp.concatenate(
            [jnp.concatenate([d2, d1], axis=1), jnp.concatenate([none, d2], axis=1)], axis=0
        )
        samples = seg_ref[pl.ds(ci, 1), :].astype(jnp.float32)
        width = out_ref.shape[1]
        pair = jnp.concatenate(
            [samples[:, s * width:(s + 1) * width] for s in range(samples.shape[1] // width)], axis=0
        )
        half_seg = pair.shape[1] // 2
        stacked = jnp.concatenate([pair[:, :half_seg], pair[:, half_seg:]], axis=0)
        stacked = stacked.astype(jnp.bfloat16)
        count = pair.shape[0]
        upper_part = jnp.dot(stacked, top, preferred_element_type=jnp.float32)
        lower_part = jnp.dot(stacked, bottom, preferred_element_type=jnp.float32)
        head = jnp.dot(previous_ref[pl.ds(ci, 1), :], top, preferred_element_type=jnp.float32)
        carried = pltpu.roll(upper_part[count:], 1, 0)
        first = lax.broadcasted_iota(jnp.int32, carried.shape, 0) == 0
        even = jnp.where(first, jnp.broadcast_to(head, carried.shape), carried) + lower_part[:count]
        odd = upper_part[:count] + lower_part[count:]
        out_ref[pl.ds(ci * count, count), :] = jnp.concatenate([even, odd], axis=1).astype(
            out_ref.dtype
        )


def whiten(fir_taps, previous, strain):
    channels, times = strain.shape
    tap_count = fir_taps.shape[1]
    count = times // SEG
    rows = pl.BlockSpec((channels, tap_count), lambda g: (0, 0))
    return pl.pallas_call(
        fir_kernel,
        out_shape=jax.ShapeDtypeStruct((channels * count, SEG), jnp.bfloat16),
        grid=(1,),
        in_specs=[rows, rows, pl.BlockSpec((channels, times), lambda g: (0, 0))],
        out_specs=pl.BlockSpec((channels * count, SEG), lambda g: (0, 0)),
        cost_estimate=pl.CostEstimate(
            flops=2 * channels * times * tap_count * 2,
            bytes_accessed=2 * strain.size * 2 + 2 * fir_taps.size * 2,
            transcendentals=0,
        ),
    )(fir_taps, previous, strain)


def shards(strain, fir_taps):
    tap_count = fir_taps.shape[1]
    channels = strain.shape[0]
    previous = shifted(strain[:, -tap_count:], "tm", 1)
    segments = whiten(fir_taps, previous, strain)
    parts = lax.axis_size("tm")
    table = make_table()
    bins = table.shape[2]
    table = jnp.asarray(
        table.reshape(SEG, 2, parts, bins // parts // 2, 2)
        .transpose(0, 2, 3, 4, 1)
        .reshape(SEG, 2 * bins)
    )
    spectra = jnp.einsum(
        "xn,nq->qx", segments, table, preferred_element_type=jnp.float32
    ).astype(jnp.bfloat16)
    pairs = bins // parts // 2
    spectra = spectra.reshape(parts, pairs, 4, spectra.shape[1])
    own = lax.all_to_all(spectra, "tm", split_axis=0, concat_axis=1, tiled=False)
    segs = own.shape[-1] // channels
    shard = own.reshape(pairs, 4 * parts, channels, segs).transpose(0, 2, 1, 3)
    shard = shard.reshape(pairs, channels, -1)
    every = lax.all_gather(shard, "chan", axis=0)
    return cross_spectra(shard, every, parts)


def cross_kernel(parts, own_ref, every_ref, out_ref):
    sources, count, channels, lanes = every_ref.shape
    segs = lanes // 4 // parts
    factor = 1.0 / (lanes // 4 * SEG)
    lane = lax.broadcasted_iota(jnp.int32, (channels, lanes), 1)
    parity = (lane // (2 * segs)) % 2
    second = (lane // segs) % 2 == 1
    for t in range(count):
        own = own_ref[t].astype(jnp.float32)
        later = pltpu.roll(own, lanes - segs, 1)
        earlier = pltpu.roll(own, segs, 1)
        swapped = jnp.where(second, -earlier, later)
        rows = []
        for part in (own, swapped):
            for b in range(2):
                rows.append(jnp.where(parity == b, part, 0.0))
        lhs = jnp.concatenate(rows, axis=0).astype(jnp.bfloat16)
        rhs = every_ref[:, t].reshape(sources * channels, lanes)
        prod = lax.dot_general(
            lhs, rhs, (((1,), (1,)), ((), ())), preferred_element_type=jnp.float32
        )
        prod = prod * factor
        for q in range(4):
            out_ref[q // 2, 2 * t + q % 2] = prod[q * channels:(q + 1) * channels]


def cross_spectra(own, every, parts):
    sources, pairs, channels, lanes = every.shape
    step = 16 if pairs % 16 == 0 else pairs
    wide = sources * channels
    return pl.pallas_call(
        functools.partial(cross_kernel, parts),
        out_shape=jax.ShapeDtypeStruct((2, 2 * pairs, channels, wide), jnp.float32),
        grid=(pairs // step,),
        in_specs=[
            pl.BlockSpec((step, channels, lanes), lambda g: (g, 0, 0)),
            pl.BlockSpec((sources, step, channels, lanes), lambda g: (0, g, 0, 0)),
        ],
        out_specs=pl.BlockSpec((2, 2 * step, channels, wide), lambda g: (0, g, 0, 0)),
        cost_estimate=pl.CostEstimate(
            flops=2 * pairs * 4 * channels * lanes * wide,
            bytes_accessed=own.size * 2 + every.size * 2 + 2 * 2 * pairs * channels * wide * 4,
            transcendentals=0,
        ),
    )(own, every)


def solution(mesh):
    placed = (P("chan", "tm"), P("chan", None))
    return jax.shard_map(
        shards, mesh=mesh, in_specs=placed, out_specs=P(None, "tm", "chan", None), check_vma=False
    )
```
